256 devices in a mesh: kx: 2 (over core), ky: 4 (over x), kz: 32 (over z, y).
Axes of the slice: x: 4, y: 4, z: 8, core: 2. Of those that a mesh axis runs over, the one named last changes fastest.
Arguments:
- populations: float32 [16, 8, 4, 64, 512], P('kx', None, None, 'ky', 'kz'), may hold values from -6 to 6
- force: float32 [16, 3, 4, 64, 512], P('kx', None, None, 'ky', 'kz'), may hold values from -3 to 3
- rate: float32 [16, 4, 64, 512], P('kx', None, 'ky', 'kz'), may hold values from 0.05 to 0.5
- tiles: bfloat16 [4, 1024, 1024], replicated, may hold values from -0.1875 to 0.1875
- send_planes: int32 [2, 4, 32, 32, 2], P('kx', 'ky', 'kz'), may hold values from 0 to 7
- recv_target: int32 [2, 4, 32, 32, 2], P('kx', 'ky', 'kz'), may hold values from 0 to 7
- recv_tile: int32 [2, 4, 32, 32, 2], P('kx', 'ky', 'kz'), may hold values from 0 to 3
- recv_count: int32 [2, 4, 32, 32], P('kx', 'ky', 'kz'), may hold values from 0 to 2, as said below
Outputs:
- final_populations: float32 [16, 8, 4, 64, 512], P('kx', None, None, 'ky', 'kz')
The draws below stay inside these ranges and needn't reach their ends.
Inputs may be any that keep to these rules, and one draw needn't show every extreme that they name: `recv_count`: every receiving brick has some source brick with all 2 slots valid, and some receiving brick has all 2 slots valid from every source brick.
All inputs are finite; a program needn't handle non-finite values.
Results may differ from the reference program's by a relative error of at most 0.0042.
Values may be sent and summed in bfloat16 or wider, within the bound.
No kernel may reach another device: no remote copies, remote signals or barrier semaphores. Data moves between devices by JAX's collectives and lax.ppermute only.
A program may use at most 128 MiB of HBM per device.

```python
import math
from functools import partial
import jax
import jax.numpy as jnp
from jax import lax

DRIVES = 8
BANDS = 4
BX = 8
BY = 16
BZ = 16
NT = 4
CAP = 2
ITERS = 2
BRICKS_X = 2
BRICKS_Y = 4
PEERS = 32
KB = 1024
NX = 16
NY = 64
NZ = 512


def draw_recv_count(key, part):
    first_key, second_key, third_key = jax.random.split(key, 3)
    shape_all = (BRICKS_X, BRICKS_Y, PEERS, PEERS)
    counts = jax.random.randint(first_key, shape_all, 0, CAP + 1)
    full_source = jax.random.randint(second_key, (BRICKS_X, BRICKS_Y, PEERS, 1), 0, PEERS)
    column = lax.broadcasted_iota(jnp.int32, shape_all, 3)
    counts = jnp.where(column == full_source, CAP, counts)
    receiver = jax.random.randint(third_key, (), 0, BRICKS_X * BRICKS_Y * PEERS)
    brick_ids = (lax.broadcasted_iota(jnp.int32, shape_all, 0) * BRICKS_Y + lax.broadcasted_iota(jnp.int32, shape_all, 1)) * PEERS + lax.broadcasted_iota(jnp.int32, shape_all, 2)
    counts = jnp.where(brick_ids == receiver, CAP, counts)
    return counts.astype(jnp.int32)


def touch_ends(values, stream_key, least, top_value):
    spot = [jax.random.randint(jax.random.fold_in(stream_key, axis), (), 0, length) for axis, length in enumerate(values.shape)]
    longest = values.shape.index(max(values.shape))
    neighbour = spot[:longest] + [(spot[longest] + 1) % values.shape[longest]] + spot[longest + 1:]
    return values.at[tuple(spot)].set(least).at[tuple(neighbour)].set(top_value)


def levels(rng, extent, pieces, least, largest):
    gain = 1.0
    for dim, blocks in pieces:
        heights = jax.random.uniform(jax.random.fold_in(jax.random.fold_in(rng, 6), dim), (blocks,), jnp.float32, least / len(pieces), largest / len(pieces))
        gain = gain * jnp.repeat(jnp.exp(heights), extent[dim] // blocks).reshape((-1,) + (1,) * (len(extent) - 1 - dim))
    return gain


def normal_values(key, dims, spread, most, pieces=(), kind=jnp.bfloat16):
    entries = jax.random.normal(key, dims, jnp.float32) * spread
    if len(pieces) > 0:
        entries = levels(key, dims, pieces, -0.22, 0.18) * entries
    return jnp.clip(entries, min=-most, max=most).astype(kind)


def setup_inputs(seed: int = 0) -> dict:
    splits = jax.random.split(jax.random.key(seed), 9)
    populations = normal_values(splits[0], (NX, DRIVES, BANDS, NY, NZ), 1.0, 6.0, ((0, 2), (3, 4), (4, 32)), jnp.float32)
    force = normal_values(splits[1], (NX, 3, BANDS, NY, NZ), 0.5, 3.0, ((0, 2), (3, 4), (4, 32)), jnp.float32)
    rate = jnp.clip(jnp.exp(math.log(0.5) - 2.3025851 * jax.random.uniform(splits[2], (NX, BANDS, NY, NZ), jnp.float32) ** levels(splits[2], (NX, BANDS, NY, NZ), ((0, 2), (2, 4), (3, 32)), -0.2, 0.2)), 0.05, 0.5)
    tiles = normal_values(splits[3], (NT, KB, KB), KB ** -0.5, 0.1875)
    send_planes = touch_ends(jax.random.randint(splits[4], (BRICKS_X, BRICKS_Y, PEERS, PEERS, CAP), 0, BX), jax.random.fold_in(splits[4], 1), 0, BX - 1).astype(jnp.int32)
    recv_target = touch_ends(jax.random.randint(splits[5], (BRICKS_X, BRICKS_Y, PEERS, PEERS, CAP), 0, BX), jax.random.fold_in(splits[5], 1), 0, BX - 1).astype(jnp.int32)
    recv_tile = touch_ends(jax.random.randint(splits[6], (BRICKS_X, BRICKS_Y, PEERS, PEERS, CAP), 0, NT), jax.random.fold_in(splits[6], 1), 0, NT - 1).astype(jnp.int32)
    recv_count = draw_recv_count(jax.random.fold_in(splits[8], 71), 0)
    return dict(populations=populations, force=force, rate=rate, tiles=tiles, send_planes=send_planes, recv_target=recv_target, recv_tile=recv_tile, recv_count=recv_count)


def derivative(values, along):
    ahead_one = jnp.roll(values, -1, along)
    behind_one = jnp.roll(values, 1, along)
    ahead_two = jnp.roll(values, -2, along)
    behind_two = jnp.roll(values, 2, along)
    return (8.0 * (ahead_one - behind_one) - (ahead_two - behind_two)) / 12.0


def brick_collision(tiles_wide, inputs):
    received, slot_count, target_ids, tile_ids = inputs
    usable = jnp.arange(CAP, dtype=jnp.int32)[None, :] < slot_count[:, None]
    tile_match = tile_ids[None, :, :] == jnp.arange(NT, dtype=jnp.int32)[:, None, None]
    plane_match = target_ids[None, :, :] == jnp.arange(BX, dtype=jnp.int32)[:, None, None]
    selector = (tile_match[:, None] & plane_match[None] & usable[None, None]).astype(jnp.float32)
    grouped = jnp.einsum("tjpc,pcdk->tjdk", selector, received.astype(jnp.float32)).astype(jnp.bfloat16)
    return jnp.einsum("tjdk,tlk->jdl", grouped.astype(jnp.float32), tiles_wide)


def reference(populations, force, rate, tiles, send_planes, recv_target, recv_tile, recv_count):
    tiles_wide = tiles.astype(jnp.float32)
    bricks = BRICKS_X * BRICKS_Y * PEERS
    current = populations
    for iteration in range(ITERS):
        drift_term = force[:, 0][:, None] * derivative(current, 0)
        drift_term = drift_term + force[:, 1][:, None] * derivative(current, 3)
        drift_term = drift_term + force[:, 2][:, None] * derivative(current, 4)
        rounded = current.astype(jnp.bfloat16)
        planes = rounded.reshape(BRICKS_X, BX, DRIVES, BANDS, BRICKS_Y, BY, PEERS, BZ)
        planes = planes.transpose(0, 4, 6, 1, 2, 3, 5, 7).reshape(BRICKS_X, BRICKS_Y, PEERS, BX, DRIVES, KB)
        chosen = send_planes.reshape(BRICKS_X, BRICKS_Y, PEERS, PEERS * CAP).astype(jnp.int32)[:, :, :, :, None, None]
        sent = jnp.take_along_axis(planes, chosen, axis=3)
        received = sent.reshape(BRICKS_X, BRICKS_Y, PEERS, PEERS, CAP, DRIVES, KB).swapaxes(2, 3)
        received = received.reshape(bricks, PEERS, CAP, DRIVES, KB)
        collision = lax.map(partial(brick_collision, tiles_wide), (received, recv_count.reshape(bricks, PEERS), recv_target.reshape(bricks, PEERS, CAP), recv_tile.reshape(bricks, PEERS, CAP)))
        collision = collision.reshape(BRICKS_X, BRICKS_Y, PEERS, BX, DRIVES, BANDS, BY, BZ)
        collision = collision.transpose(0, 3, 4, 5, 1, 6, 2, 7).reshape(NX, DRIVES, BANDS, NY, NZ)
        current = current - drift_term + collision - rate[:, None] * current
    return current
```

```python
import jax
import jax.numpy as jnp
from jax import lax
from jax.experimental import pallas as pl
from jax.experimental.pallas import tpu as pltpu
from jax.sharding import PartitionSpec as P

ITERS = 2
F32 = jnp.float32
BF16 = jnp.bfloat16


def _split3(h):
    hi = h.astype(BF16)
    rest = h - hi.astype(F32)
    mid = rest.astype(BF16)
    lo = (rest - mid.astype(F32)).astype(BF16)
    return hi, mid, lo


def _exact_dot(h, m):
    hi, mid, lo = _split3(h)
    out = jnp.dot(hi, m, preferred_element_type=F32)
    out = out + jnp.dot(mid, m, preferred_element_type=F32)
    return out + jnp.dot(lo, m, preferred_element_type=F32)


def _select(kind, shape, k_axis):
    k = lax.broadcasted_iota(jnp.int32, shape, k_axis)
    c = lax.broadcasted_iota(jnp.int32, shape, 1 - k_axis)
    z = k & 15
    y = (k >> 4) & 15
    g = k >> 4
    b = k >> 8
    if kind == "z_lo":
        hit = (z < 2) & (c == g * 2 + z)
    elif kind == "z_hi":
        hit = (z >= 14) & (c == g * 2 + z - 14)
    elif kind == "y_lo":
        hit = (y < 2) & (c == b * 32 + y * 16 + z)
    else:
        hit = (y >= 14) & (c == b * 32 + (y - 14) * 16 + z)
    return jnp.where(hit, 1.0, 0.0).astype(BF16)


def _compress(cur, kind):
    lanes = cur.shape[1]
    return _exact_dot(cur, _select(kind, (lanes, 128), 0))


def _expand(h, kind, lanes):
    return _exact_dot(h, _select(kind, (128, lanes), 1))


def _emit_halos(cur, rnd_ref, zlo_ref, zhi_ref, ylo_ref, yhi_ref):
    rnd_ref[...] = cur.astype(BF16)
    zlo_ref[...] = _compress(cur, "z_lo")
    zhi_ref[...] = _compress(cur, "z_hi")
    ylo_ref[...] = _compress(cur, "y_lo")
    yhi_ref[...] = _compress(cur, "y_hi")


def _prep_kernel(cur_ref, rnd_ref, zlo_ref, zhi_ref, ylo_ref, yhi_ref):
    _emit_halos(cur_ref[...], rnd_ref, zlo_ref, zhi_ref, ylo_ref, yhi_ref)


def _finish_kernel(p_ref, coll_ref, q_ref, cur_ref, rnd_ref, zlo_ref, zhi_ref, ylo_ref, yhi_ref):
    cur = (p_ref[...] + coll_ref[...]) - q_ref[...]
    cur_ref[...] = cur
    _emit_halos(cur, rnd_ref, zlo_ref, zhi_ref, ylo_ref, yhi_ref)


def _deriv(a1, m1, a2, m2):
    return (8.0 * (a1 - m1) - (a2 - m2)) / 12.0


def _drift_kernel(cur_ref, xlo_ref, xhi_ref, hyp_ref, hym_ref, hzp_ref, hzm_ref,
                  fx_ref, fy_ref, fz_ref, rate_ref, p_ref, q_ref, ext_ref):
    rows, lanes = cur_ref.shape
    cur = cur_ref[...]
    ext_ref[0:16, :] = xlo_ref[...]
    ext_ref[16:16 + rows, :] = cur
    ext_ref[16 + rows:32 + rows, :] = xhi_ref[...]
    dx = _deriv(ext_ref[24:24 + rows, :], ext_ref[8:8 + rows, :],
                ext_ref[32:32 + rows, :], ext_ref[0:rows, :])

    k = lax.broadcasted_iota(jnp.int32, (rows, lanes), 1)
    z = k & 15
    y = (k >> 4) & 15

    eyp = _expand(hyp_ref[...], "y_hi", lanes)
    eym = _expand(hym_ref[...], "y_lo", lanes)
    yp1 = jnp.where(y == 15, pltpu.roll(eyp, 16, 1), pltpu.roll(cur, lanes - 16, 1))
    yp2 = jnp.where(y >= 14, eyp, pltpu.roll(cur, lanes - 32, 1))
    ym1 = jnp.where(y == 0, pltpu.roll(eym, lanes - 16, 1), pltpu.roll(cur, 16, 1))
    ym2 = jnp.where(y <= 1, eym, pltpu.roll(cur, 32, 1))
    dy = _deriv(yp1, ym1, yp2, ym2)

    ezp = _expand(hzp_ref[...], "z_hi", lanes)
    ezm = _expand(hzm_ref[...], "z_lo", lanes)
    zp1 = jnp.where(z == 15, pltpu.roll(ezp, 1, 1), pltpu.roll(cur, lanes - 1, 1))
    zp2 = jnp.where(z >= 14, ezp, pltpu.roll(cur, lanes - 2, 1))
    zm1 = jnp.where(z == 0, pltpu.roll(ezm, lanes - 1, 1), pltpu.roll(cur, 1, 1))
    zm2 = jnp.where(z <= 1, ezm, pltpu.roll(cur, 2, 1))
    dz = _deriv(zp1, zm1, zp2, zm2)

    drift = fx_ref[...] * dx
    drift = drift + fy_ref[...] * dy
    drift = drift + fz_ref[...] * dz
    p_ref[...] = cur - drift
    q_ref[...] = rate_ref[...] * cur


def _shapes(rows, lanes):
    plane = jax.ShapeDtypeStruct((rows, lanes), F32)
    halo = jax.ShapeDtypeStruct((rows, 128), F32)
    return [jax.ShapeDtypeStruct((rows, lanes), BF16), halo, halo, halo, halo], plane


def _prep(cur):
    rest, _ = _shapes(*cur.shape)
    return pl.pallas_call(_prep_kernel, out_shape=rest)(cur)


def _finish(p, coll, q):
    rest, plane = _shapes(*p.shape)
    outs = pl.pallas_call(_finish_kernel, out_shape=[plane] + rest)(p, coll, q)
    return outs[0], outs[1:]


def _drift(cur, xlo, xhi, hyp, hym, hzp, hzm, fx, fy, fz, rate):
    rows, lanes = cur.shape
    plane = jax.ShapeDtypeStruct((rows, lanes), F32)
    return pl.pallas_call(
        _drift_kernel,
        out_shape=[plane, plane],
        scratch_shapes=[pltpu.VMEM((rows + 32, lanes), F32)],
    )(cur, xlo, xhi, hyp, hym, hzp, hzm, fx, fy, fz, rate)


def _ring(axis):
    size = lax.axis_size(axis)
    up = [(i, (i + 1) % size) for i in range(size)]
    down = [(j, i) for i, j in up]
    return up, down


def per_device(populations, force, rate, tiles, send_planes, recv_target, recv_tile, recv_count):
    width_x, drive_count, band_count, width_y, width_z = populations.shape
    rows = width_x * drive_count
    lanes = band_count * width_y * width_z
    peer_count = lax.axis_size("kz")
    slot_cap = send_planes.shape[-1]
    tile_count = tiles.shape[0]
    plane_list = send_planes.reshape(peer_count * slot_cap)
    slot_count = recv_count.reshape(peer_count)
    target_ids = recv_target.reshape(peer_count, slot_cap)
    tile_ids = recv_tile.reshape(peer_count, slot_cap)
    usable = lax.broadcasted_iota(jnp.int32, (peer_count, slot_cap), 1) < slot_count[:, None]
    tile_match = (
        tile_ids[None, None] == jnp.arange(tile_count, dtype=jnp.int32)[:, None, None, None]
    )
    plane_match = (
        target_ids[None, None] == jnp.arange(width_x, dtype=jnp.int32)[None, :, None, None]
    )
    selector = (tile_match & plane_match & usable[None, None]).astype(BF16)
    selector = selector.reshape(tile_count * width_x, peer_count * slot_cap)

    def spread(a):
        a = a.reshape(width_x, 1, lanes)
        return jnp.broadcast_to(a, (width_x, drive_count, lanes)).reshape(rows, lanes)

    fx = spread(force[:, 0])
    fy = spread(force[:, 1])
    fz = spread(force[:, 2])
    rate_wide = spread(rate)

    up_x, down_x = _ring("kx")
    up_y, down_y = _ring("ky")
    up_z, down_z = _ring("kz")

    cur = populations.reshape(rows, lanes)
    rnd, zlo, zhi, ylo, yhi = _prep(cur)
    for iteration in range(ITERS):
        xlo = lax.ppermute(cur[rows - 16:], "kx", up_x)
        xhi = lax.ppermute(cur[:16], "kx", down_x)
        hym = lax.ppermute(yhi, "ky", up_y)
        hyp = lax.ppermute(ylo, "ky", down_y)
        hzm = lax.ppermute(zhi, "kz", up_z)
        hzp = lax.ppermute(zlo, "kz", down_z)
        plane_rows = rnd.reshape(width_x, drive_count, lanes)
        outgoing = plane_rows[plane_list].reshape(peer_count, slot_cap, drive_count, lanes)
        incoming = lax.all_to_all(outgoing, "kz", split_axis=0, concat_axis=0, tiled=True)
        p, q = _drift(cur, xlo, xhi, hyp, hym, hzp, hzm, fx, fy, fz, rate_wide)
        summed = lax.dot_general(
            selector,
            incoming.reshape(peer_count * slot_cap, drive_count, lanes),
            (((1,), (0,)), ((), ())),
            preferred_element_type=F32,
        )
        grouped = summed.astype(BF16).reshape(tile_count, rows, lanes)
        coll = lax.dot_general(
            grouped, tiles, (((0, 2), (0, 2)), ((), ())), preferred_element_type=F32
        )
        if iteration + 1 < ITERS:
            cur, (rnd, zlo, zhi, ylo, yhi) = _finish(p, coll, q)
        else:
            cur = (p + coll) - q
    return cur.reshape(width_x, drive_count, band_count, width_y, width_z)


def solution(mesh):
    placed = (
        P("kx", None, None, "ky", "kz"),
        P("kx", None, None, "ky", "kz"),
        P("kx", None, "ky", "kz"),
        P(),
        P("kx", "ky", "kz", None, None),
        P("kx", "ky", "kz", None, None),
        P("kx", "ky", "kz", None, None),
        P("kx", "ky", "kz", None),
    )
    return jax.shard_map(
        per_device,
        mesh=mesh,
        in_specs=placed,
        out_specs=P("kx", None, None, "ky", "kz"),
        check_vma=False,
    )
```

```python
import functools

import jax
import jax.numpy as jnp
from jax import lax
from jax.experimental import pallas as pl
from jax.experimental.pallas import tpu as pltpu
from jax.sharding import PartitionSpec as P

ITERS = 2
F32 = jnp.float32
BF16 = jnp.bfloat16


def _split3(h):
    hi = h.astype(BF16)
    rest = h - hi.astype(F32)
    mid = rest.astype(BF16)
    lo = (rest - mid.astype(F32)).astype(BF16)
    return hi, mid, lo


def _exact_dot(h, m):
    hi, mid, lo = _split3(h)
    out = jnp.dot(hi, m, preferred_element_type=F32)
    out = out + jnp.dot(mid, m, preferred_element_type=F32)
    return out + jnp.dot(lo, m, preferred_element_type=F32)


def _select(kind, shape, k_axis):
    k = lax.broadcasted_iota(jnp.int32, shape, k_axis)
    c = lax.broadcasted_iota(jnp.int32, shape, 1 - k_axis)
    z = k & 15
    y = (k >> 4) & 15
    g = k >> 4
    b = k >> 8
    if kind == "z_lo":
        hit = (z < 2) & (c == g * 2 + z)
    elif kind == "z_hi":
        hit = (z >= 14) & (c == g * 2 + z - 14)
    elif kind == "y_lo":
        hit = (y < 2) & (c == b * 32 + y * 16 + z)
    else:
        hit = (y >= 14) & (c == b * 32 + (y - 14) * 16 + z)
    return jnp.where(hit, 1.0, 0.0).astype(BF16)


def _compress(cur, kind):
    lanes = cur.shape[1]
    return _exact_dot(cur, _select(kind, (lanes, 128), 0))


def _expand(h, kind, lanes):
    return _exact_dot(h, _select(kind, (128, lanes), 1))


def _emit_halos(cur, zlo_ref, zhi_ref, ylo_ref, yhi_ref):
    zlo_ref[...] = _compress(cur, "z_lo")
    zhi_ref[...] = _compress(cur, "z_hi")
    ylo_ref[...] = _compress(cur, "y_lo")
    yhi_ref[...] = _compress(cur, "y_hi")


def _emit_send(plist_ref, cur_ref, snd_ref):
    peers, both, _ = snd_ref.shape
    slot_cap = both // 8
    for s in range(peers):
        parts = []
        for c in range(slot_cap):
            plane = plist_ref[s * slot_cap + c]
            parts.append(cur_ref[pl.ds(pl.multiple_of(plane * 8, 8), 8), :])
        snd_ref[s] = jnp.concatenate(parts, axis=0).astype(BF16)


def _prep_kernel(plist_ref, cur_ref, snd_ref, zlo_ref, zhi_ref, ylo_ref, yhi_ref):
    _emit_send(plist_ref, cur_ref, snd_ref)
    _emit_halos(cur_ref[...], zlo_ref, zhi_ref, ylo_ref, yhi_ref)


def _finish_kernel(last, plist_ref, sel_ref, inc_ref, p_ref, q_ref, w_ref, *refs):
    if last:
        cur_ref, g_scr, acc_scr = refs
    else:
        cur_ref, snd_ref, zlo_ref, zhi_ref, ylo_ref, yhi_ref, g_scr, acc_scr = refs
    t = pl.program_id(0)
    rows = p_ref.shape[0]

    @pl.when(t == 0)
    def _():
        summed = jnp.dot(sel_ref[...], inc_ref[...], preferred_element_type=F32)
        g_scr[...] = summed.astype(BF16)
        acc_scr[...] = jnp.zeros_like(acc_scr)

    grouped = g_scr[pl.ds(pl.multiple_of(t * rows, rows), rows), :]
    acc_scr[...] += lax.dot_general(
        grouped, w_ref[0], (((1,), (1,)), ((), ())), preferred_element_type=F32
    )

    @pl.when(t == pl.num_programs(0) - 1)
    def _():
        cur = (p_ref[...] + acc_scr[...]) - q_ref[...]
        cur_ref[...] = cur
        if not last:
            _emit_halos(cur, zlo_ref, zhi_ref, ylo_ref, yhi_ref)
            _emit_send(plist_ref, cur_ref, snd_ref)


def _deriv(a1, m1, a2, m2):
    return (8.0 * (a1 - m1) - (a2 - m2)) / 12.0


def _drift_kernel(cur_ref, xlo_ref, xhi_ref, hyp_ref, hym_ref, hzp_ref, hzm_ref,
                  fx_ref, fy_ref, fz_ref, rate_ref, p_ref, q_ref, ext_ref):
    rows, lanes = cur_ref.shape
    cur = cur_ref[...]
    ext_ref[0:16, :] = xlo_ref[...]
    ext_ref[16:16 + rows, :] = cur
    ext_ref[16 + rows:32 + rows, :] = xhi_ref[...]
    dx = _deriv(ext_ref[24:24 + rows, :], ext_ref[8:8 + rows, :],
                ext_ref[32:32 + rows, :], ext_ref[0:rows, :])

    k = lax.broadcasted_iota(jnp.int32, (rows, lanes), 1)
    z = k & 15
    y = (k >> 4) & 15

    eyp = _expand(hyp_ref[...], "y_hi", lanes)
    eym = _expand(hym_ref[...], "y_lo", lanes)
    yp1 = jnp.where(y == 15, pltpu.roll(eyp, 16, 1), pltpu.roll(cur, lanes - 16, 1))
    yp2 = jnp.where(y >= 14, eyp, pltpu.roll(cur, lanes - 32, 1))
    ym1 = jnp.where(y == 0, pltpu.roll(eym, lanes - 16, 1), pltpu.roll(cur, 16, 1))
    ym2 = jnp.where(y <= 1, eym, pltpu.roll(cur, 32, 1))
    dy = _deriv(yp1, ym1, yp2, ym2)

    ezp = _expand(hzp_ref[...], "z_hi", lanes)
    ezm = _expand(hzm_ref[...], "z_lo", lanes)
    zp1 = jnp.where(z == 15, pltpu.roll(ezp, 1, 1), pltpu.roll(cur, lanes - 1, 1))
    zp2 = jnp.where(z >= 14, ezp, pltpu.roll(cur, lanes - 2, 1))
    zm1 = jnp.where(z == 0, pltpu.roll(ezm, lanes - 1, 1), pltpu.roll(cur, 1, 1))
    zm2 = jnp.where(z <= 1, ezm, pltpu.roll(cur, 2, 1))
    dz = _deriv(zp1, zm1, zp2, zm2)

    drift = fx_ref[...] * dx
    drift = drift + fy_ref[...] * dy
    drift = drift + fz_ref[...] * dz
    p_ref[...] = cur - drift
    q_ref[...] = rate_ref[...] * cur


def _full(shape):
    zeros = (0,) * len(shape)
    return pl.BlockSpec(shape, lambda *_: zeros)


def _rest_shapes(rows, lanes, peers, both):
    halo = jax.ShapeDtypeStruct((rows, 128), F32)
    snd = jax.ShapeDtypeStruct((peers, both, lanes), BF16)
    return [snd, halo, halo, halo, halo]


def _prep(plist, cur, peers, both):
    rows, lanes = cur.shape
    shapes = _rest_shapes(rows, lanes, peers, both)
    return pl.pallas_call(
        _prep_kernel,
        out_shape=shapes,
        grid_spec=pltpu.PrefetchScalarGridSpec(
            num_scalar_prefetch=1,
            grid=(1,),
            in_specs=[_full(cur.shape)],
            out_specs=[_full(x.shape) for x in shapes],
        ),
    )(plist, cur)


def _finish(last, plist, sel, inc, p, q, tiles, peers, both):
    rows, lanes = p.shape
    tile_count = tiles.shape[0]
    shapes = [jax.ShapeDtypeStruct((rows, lanes), F32)]
    if not last:
        shapes += _rest_shapes(rows, lanes, peers, both)
    outs = pl.pallas_call(
        functools.partial(_finish_kernel, last),
        out_shape=shapes,
        grid_spec=pltpu.PrefetchScalarGridSpec(
            num_scalar_prefetch=1,
            grid=(tile_count,),
            in_specs=[
                _full(sel.shape),
                _full(inc.shape),
                _full(p.shape),
                _full(q.shape),
                pl.BlockSpec((1,) + tiles.shape[1:], lambda t, *_: (t, 0, 0)),
            ],
            out_specs=[_full(x.shape) for x in shapes],
            scratch_shapes=[
                pltpu.VMEM((tile_count * rows, lanes), BF16),
                pltpu.VMEM((rows, lanes), F32),
            ],
        ),
        compiler_params=pltpu.CompilerParams(dimension_semantics=("arbitrary",)),
    )(plist, sel, inc, p, q, tiles)
    return outs[0], outs[1:]


def _drift(cur, xlo, xhi, hyp, hym, hzp, hzm, fx, fy, fz, rate):
    rows, lanes = cur.shape
    plane = jax.ShapeDtypeStruct((rows, lanes), F32)
    return pl.pallas_call(
        _drift_kernel,
        out_shape=[plane, plane],
        scratch_shapes=[pltpu.VMEM((rows + 32, lanes), F32)],
    )(cur, xlo, xhi, hyp, hym, hzp, hzm, fx, fy, fz, rate)


def _ring(axis):
    size = lax.axis_size(axis)
    up = [(i, (i + 1) % size) for i in range(size)]
    down = [(j, i) for i, j in up]
    return up, down


def per_device(populations, force, rate, tiles, send_planes, recv_target, recv_tile, recv_count):
    width_x, drive_count, band_count, width_y, width_z = populations.shape
    rows = width_x * drive_count
    lanes = band_count * width_y * width_z
    peer_count = lax.axis_size("kz")
    slot_cap = send_planes.shape[-1]
    tile_count = tiles.shape[0]
    plane_list = send_planes.reshape(peer_count * slot_cap)
    slot_count = recv_count.reshape(peer_count)
    target_ids = recv_target.reshape(peer_count, slot_cap)
    tile_ids = recv_tile.reshape(peer_count, slot_cap)
    usable = lax.broadcasted_iota(jnp.int32, (peer_count, slot_cap), 1) < slot_count[:, None]
    tile_match = (
        tile_ids[None, None] == jnp.arange(tile_count, dtype=jnp.int32)[:, None, None, None]
    )
    plane_match = (
        target_ids[None, None] == jnp.arange(width_x, dtype=jnp.int32)[None, :, None, None]
    )
    selector = (tile_match & plane_match & usable[None, None]).astype(BF16)
    selector = selector.reshape(tile_count * width_x, peer_count * slot_cap)
    eye = jnp.eye(drive_count, dtype=BF16)
    sel_big = (selector[:, None, :, None] * eye[None, :, None, :]).reshape(
        tile_count * width_x * drive_count, peer_count * slot_cap * drive_count
    )
    both = slot_cap * drive_count

    def spread(a):
        a = a.reshape(width_x, 1, lanes)
        return jnp.broadcast_to(a, (width_x, drive_count, lanes)).reshape(rows, lanes)

    fx = spread(force[:, 0])
    fy = spread(force[:, 1])
    fz = spread(force[:, 2])
    rate_wide = spread(rate)

    up_x, down_x = _ring("kx")
    up_y, down_y = _ring("ky")
    up_z, down_z = _ring("kz")

    cur = populations.reshape(rows, lanes)
    snd, zlo, zhi, ylo, yhi = _prep(plane_list, cur, peer_count, both)
    for iteration in range(ITERS):
        last = iteration + 1 == ITERS
        xlo = lax.ppermute(cur[rows - 16:], "kx", up_x)
        xhi = lax.ppermute(cur[:16], "kx", down_x)
        hym = lax.ppermute(yhi, "ky", up_y)
        hyp = lax.ppermute(ylo, "ky", down_y)
        hzm = lax.ppermute(zhi, "kz", up_z)
        hzp = lax.ppermute(zlo, "kz", down_z)
        incoming = lax.all_to_all(snd, "kz", split_axis=0, concat_axis=0, tiled=True)
        p, q = _drift(cur, xlo, xhi, hyp, hym, hzp, hzm, fx, fy, fz, rate_wide)
        inc = incoming.reshape(peer_count * both, lanes)
        cur, rest = _finish(last, plane_list, sel_big, inc, p, q, tiles, peer_count, both)
        if not last:
            snd, zlo, zhi, ylo, yhi = rest
    return cur.reshape(width_x, drive_count, band_count, width_y, width_z)


def solution(mesh):
    placed = (
        P("kx", None, None, "ky", "kz"),
        P("kx", None, None, "ky", "kz"),
        P("kx", None, "ky", "kz"),
        P(),
        P("kx", "ky", "kz", None, None),
        P("kx", "ky", "kz", None, None),
        P("kx", "ky", "kz", None, None),
        P("kx", "ky", "kz", None),
    )
    return jax.shard_map(
        per_device,
        mesh=mesh,
        in_specs=placed,
        out_specs=P("kx", None, None, "ky", "kz"),
        check_vma=False,
    )
```

```python
import functools

import jax
import jax.numpy as jnp
from jax import lax
from jax.experimental import pallas as pl
from jax.experimental.pallas import tpu as pltpu
from jax.sharding import PartitionSpec as P

ITERS = 2
F32 = jnp.float32
BF16 = jnp.bfloat16


def _split3(h):
    hi = h.astype(BF16)
    rest = h - hi.astype(F32)
    mid = rest.astype(BF16)
    lo = (rest - mid.astype(F32)).astype(BF16)
    return hi, mid, lo


def _exact_dot(h, m):
    hi, mid, lo = _split3(h)
    out = jnp.dot(hi, m, preferred_element_type=F32)
    out = out + jnp.dot(mid, m, preferred_element_type=F32)
    return out + jnp.dot(lo, m, preferred_element_type=F32)


def _select(kind, shape, k_axis):
    k = lax.broadcasted_iota(jnp.int32, shape, k_axis)
    c = lax.broadcasted_iota(jnp.int32, shape, 1 - k_axis)
    z = k & 15
    y = (k >> 4) & 15
    g = k >> 4
    b = k >> 8
    if kind == "z_lo":
        hit = (z < 2) & (c == g * 2 + z)
    elif kind == "z_hi":
        hit = (z >= 14) & (c == g * 2 + z - 14)
    elif kind == "y_lo":
        hit = (y < 2) & (c == b * 32 + y * 16 + z)
    else:
        hit = (y >= 14) & (c == b * 32 + (y - 14) * 16 + z)
    return jnp.where(hit, 1.0, 0.0).astype(BF16)


def _compress(cur, kind):
    lanes = cur.shape[1]
    return _exact_dot(cur, _select(kind, (lanes, 128), 0))


def _expand(h, kind, lanes):
    return _exact_dot(h, _select(kind, (128, lanes), 1))


def _emit_halos(cur, zlo_ref, zhi_ref, ylo_ref, yhi_ref):
    zlo_ref[...] = _compress(cur, "z_lo")
    zhi_ref[...] = _compress(cur, "z_hi")
    ylo_ref[...] = _compress(cur, "y_lo")
    yhi_ref[...] = _compress(cur, "y_hi")


def _emit_send(plist_ref, cur_ref, snd_ref):
    peers, both, _ = snd_ref.shape
    slot_cap = both // 8
    for s in range(peers):
        parts = []
        for c in range(slot_cap):
            plane = plist_ref[s * slot_cap + c]
            parts.append(cur_ref[pl.ds(pl.multiple_of(plane * 8, 8), 8), :])
        snd_ref[s] = jnp.concatenate(parts, axis=0).astype(BF16)


def _send_kernel(plist_ref, cur_ref, snd_ref):
    _emit_send(plist_ref, cur_ref, snd_ref)


def _halo_kernel(cur_ref, zlo_ref, zhi_ref, ylo_ref, yhi_ref):
    _emit_halos(cur_ref[...], zlo_ref, zhi_ref, ylo_ref, yhi_ref)


def _finish_kernel(last, plist_ref, sel_ref, inc_ref, p_ref, q_ref, w_ref, *refs):
    if last:
        cur_ref, g_scr, acc_scr = refs
    else:
        cur_ref, snd_ref, g_scr, acc_scr = refs
    t = pl.program_id(0)
    rows = p_ref.shape[0]

    @pl.when(t == 0)
    def _():
        summed = jnp.dot(sel_ref[...], inc_ref[...], preferred_element_type=F32)
        g_scr[...] = summed.astype(BF16)
        acc_scr[...] = jnp.zeros_like(acc_scr)

    grouped = g_scr[pl.ds(pl.multiple_of(t * rows, rows), rows), :]
    acc_scr[...] += lax.dot_general(
        grouped, w_ref[0], (((1,), (1,)), ((), ())), preferred_element_type=F32
    )

    @pl.when(t == pl.num_programs(0) - 1)
    def _():
        cur = (p_ref[...] + acc_scr[...]) - q_ref[...]
        cur_ref[...] = cur
        if not last:
            _emit_send(plist_ref, cur_ref, snd_ref)


def _deriv(a1, m1, a2, m2):
    return (8.0 * (a1 - m1) - (a2 - m2)) / 12.0


def _drift_kernel(cur_ref, xlo_ref, xhi_ref, hyp_ref, hym_ref, hzp_ref, hzm_ref,
                  fx_ref, fy_ref, fz_ref, rate_ref, p_ref, q_ref, ext_ref):
    rows, lanes = cur_ref.shape
    cur = cur_ref[...]
    ext_ref[0:16, :] = xlo_ref[...]
    ext_ref[16:16 + rows, :] = cur
    ext_ref[16 + rows:32 + rows, :] = xhi_ref[...]
    dx = _deriv(ext_ref[24:24 + rows, :], ext_ref[8:8 + rows, :],
                ext_ref[32:32 + rows, :], ext_ref[0:rows, :])

    k = lax.broadcasted_iota(jnp.int32, (rows, lanes), 1)
    z = k & 15
    y = (k >> 4) & 15

    eyp = _expand(hyp_ref[...], "y_hi", lanes)
    eym = _expand(hym_ref[...], "y_lo", lanes)
    yp1 = jnp.where(y == 15, pltpu.roll(eyp, 16, 1), pltpu.roll(cur, lanes - 16, 1))
    yp2 = jnp.where(y >= 14, eyp, pltpu.roll(cur, lanes - 32, 1))
    ym1 = jnp.where(y == 0, pltpu.roll(eym, lanes - 16, 1), pltpu.roll(cur, 16, 1))
    ym2 = jnp.where(y <= 1, eym, pltpu.roll(cur, 32, 1))
    dy = _deriv(yp1, ym1, yp2, ym2)

    ezp = _expand(hzp_ref[...], "z_hi", lanes)
    ezm = _expand(hzm_ref[...], "z_lo", lanes)
    zp1 = jnp.where(z == 15, pltpu.roll(ezp, 1, 1), pltpu.roll(cur, lanes - 1, 1))
    zp2 = jnp.where(z >= 14, ezp, pltpu.roll(cur, lanes - 2, 1))
    zm1 = jnp.where(z == 0, pltpu.roll(ezm, lanes - 1, 1), pltpu.roll(cur, 1, 1))
    zm2 = jnp.where(z <= 1, ezm, pltpu.roll(cur, 2, 1))
    dz = _deriv(zp1, zm1, zp2, zm2)

    drift = fx_ref[...] * dx
    drift = drift + fy_ref[...] * dy
    drift = drift + fz_ref[...] * dz
    p_ref[...] = cur - drift
    q_ref[...] = rate_ref[...] * cur


def _full(shape):
    zeros = (0,) * len(shape)
    return pl.BlockSpec(shape, lambda *_: zeros)


def _send_shape(lanes, peers, both):
    return jax.ShapeDtypeStruct((peers, both, lanes), BF16)


def _send(plist, cur, peers, both):
    shape = _send_shape(cur.shape[1], peers, both)
    return pl.pallas_call(
        _send_kernel,
        out_shape=shape,
        grid_spec=pltpu.PrefetchScalarGridSpec(
            num_scalar_prefetch=1,
            grid=(1,),
            in_specs=[_full(cur.shape)],
            out_specs=_full(shape.shape),
        ),
    )(plist, cur)


def _halos(cur):
    halo = jax.ShapeDtypeStruct((cur.shape[0], 128), F32)
    return pl.pallas_call(_halo_kernel, out_shape=[halo] * 4)(cur)


def _finish(last, plist, sel, inc, p, q, tiles, peers, both):
    rows, lanes = p.shape
    tile_count = tiles.shape[0]
    shapes = [jax.ShapeDtypeStruct((rows, lanes), F32)]
    if not last:
        shapes.append(_send_shape(lanes, peers, both))
    outs = pl.pallas_call(
        functools.partial(_finish_kernel, last),
        out_shape=shapes,
        grid_spec=pltpu.PrefetchScalarGridSpec(
            num_scalar_prefetch=1,
            grid=(tile_count,),
            in_specs=[
                _full(sel.shape),
                _full(inc.shape),
                _full(p.shape),
                _full(q.shape),
                pl.BlockSpec((1,) + tiles.shape[1:], lambda t, *_: (t, 0, 0)),
            ],
            out_specs=[_full(x.shape) for x in shapes],
            scratch_shapes=[
                pltpu.VMEM((tile_count * rows, lanes), BF16),
                pltpu.VMEM((rows, lanes), F32),
            ],
        ),
        compiler_params=pltpu.CompilerParams(dimension_semantics=("arbitrary",)),
    )(plist, sel, inc, p, q, tiles)
    return outs[0], outs[1:]


def _drift(cur, xlo, xhi, hyp, hym, hzp, hzm, fx, fy, fz, rate):
    rows, lanes = cur.shape
    plane = jax.ShapeDtypeStruct((rows, lanes), F32)
    return pl.pallas_call(
        _drift_kernel,
        out_shape=[plane, plane],
        scratch_shapes=[pltpu.VMEM((rows + 32, lanes), F32)],
    )(cur, xlo, xhi, hyp, hym, hzp, hzm, fx, fy, fz, rate)


def _ring(axis):
    size = lax.axis_size(axis)
    up = [(i, (i + 1) % size) for i in range(size)]
    down = [(j, i) for i, j in up]
    return up, down


def per_device(populations, force, rate, tiles, send_planes, recv_target, recv_tile, recv_count):
    width_x, drive_count, band_count, width_y, width_z = populations.shape
    rows = width_x * drive_count
    lanes = band_count * width_y * width_z
    peer_count = lax.axis_size("kz")
    slot_cap = send_planes.shape[-1]
    tile_count = tiles.shape[0]
    plane_list = send_planes.reshape(peer_count * slot_cap)
    slot_count = recv_count.reshape(peer_count)
    target_ids = recv_target.reshape(peer_count, slot_cap)
    tile_ids = recv_tile.reshape(peer_count, slot_cap)
    usable = lax.broadcasted_iota(jnp.int32, (peer_count, slot_cap), 1) < slot_count[:, None]
    tile_match = (
        tile_ids[None, None] == jnp.arange(tile_count, dtype=jnp.int32)[:, None, None, None]
    )
    plane_match = (
        target_ids[None, None] == jnp.arange(width_x, dtype=jnp.int32)[None, :, None, None]
    )
    selector = (tile_match & plane_match & usable[None, None]).astype(BF16)
    flat_tile = jnp.repeat(tile_ids.reshape(-1), drive_count)
    flat_target = jnp.repeat(target_ids.reshape(-1), drive_count)
    flat_usable = jnp.repeat(usable.reshape(-1), drive_count)
    big_rows = tile_count * width_x * drive_count
    big_cols = peer_count * slot_cap * drive_count
    r = lax.broadcasted_iota(jnp.int32, (big_rows, big_cols), 0)
    col = lax.broadcasted_iota(jnp.int32, (big_rows, big_cols), 1)
    hit = (r // (width_x * drive_count)) == flat_tile[None, :]
    hit = hit & (((r // drive_count) % width_x) == flat_target[None, :])
    hit = hit & flat_usable[None, :] & ((r % drive_count) == (col % drive_count))
    sel_big = hit.astype(BF16)
    both = slot_cap * drive_count

    def spread(a):
        a = a.reshape(width_x, 1, lanes)
        return jnp.broadcast_to(a, (width_x, drive_count, lanes)).reshape(rows, lanes)

    fx = spread(force[:, 0])
    fy = spread(force[:, 1])
    fz = spread(force[:, 2])
    rate_wide = spread(rate)

    up_x, down_x = _ring("kx")
    up_y, down_y = _ring("ky")
    up_z, down_z = _ring("kz")

    cur = populations.reshape(rows, lanes)
    snd = _send(plane_list, cur, peer_count, both)
    for iteration in range(ITERS):
        last = iteration + 1 == ITERS
        zlo, zhi, ylo, yhi = _halos(cur)
        xlo = lax.ppermute(cur[rows - 16:], "kx", up_x)
        xhi = lax.ppermute(cur[:16], "kx", down_x)
        hym = lax.ppermute(yhi, "ky", up_y)
        hyp = lax.ppermute(ylo, "ky", down_y)
        hzm = lax.ppermute(zhi, "kz", up_z)
        hzp = lax.ppermute(zlo, "kz", down_z)
        incoming = lax.all_to_all(snd, "kz", split_axis=0, concat_axis=0, tiled=True)
        p, q = _drift(cur, xlo, xhi, hyp, hym, hzp, hzm, fx, fy, fz, rate_wide)
        inc = incoming.reshape(peer_count * both, lanes)
        cur, rest = _finish(last, plane_list, sel_big, inc, p, q, tiles, peer_count, both)
        if not last:
            (snd,) = rest
    return cur.reshape(width_x, drive_count, band_count, width_y, width_z)


def solution(mesh):
    placed = (
        P("kx", None, None, "ky", "kz"),
        P("kx", None, None, "ky", "kz"),
        P("kx", None, "ky", "kz"),
        P(),
        P("kx", "ky", "kz", None, None),
        P("kx", "ky", "kz", None, None),
        P("kx", "ky", "kz", None, None),
        P("kx", "ky", "kz", None),
    )
    return jax.shard_map(
        per_device,
        mesh=mesh,
        in_specs=placed,
        out_specs=P("kx", None, None, "ky", "kz"),
        check_vma=False,
    )
```

```python
import functools

import jax
import jax.numpy as jnp
from jax import lax
from jax.experimental import pallas as pl
from jax.experimental.pallas import tpu as pltpu
from jax.sharding import PartitionSpec as P

ITERS = 2
F32 = jnp.float32
BF16 = jnp.bfloat16


def _split3(h):
    hi = h.astype(BF16)
    rest = h - hi.astype(F32)
    mid = rest.astype(BF16)
    lo = (rest - mid.astype(F32)).astype(BF16)
    return hi, mid, lo


def _exact_dot(h, m):
    hi, mid, lo = _split3(h)
    out = jnp.dot(hi, m, preferred_element_type=F32)
    out = out + jnp.dot(mid, m, preferred_element_type=F32)
    return out + jnp.dot(lo, m, preferred_element_type=F32)


def _select(kind, shape, k_axis):
    k = lax.broadcasted_iota(jnp.int32, shape, k_axis)
    c = lax.broadcasted_iota(jnp.int32, shape, 1 - k_axis)
    z = k & 15
    y = (k >> 4) & 15
    g = k >> 4
    b = k >> 8
    if kind == "z_lo":
        hit = (z < 2) & (c == g * 2 + z)
    elif kind == "z_hi":
        hit = (z >= 14) & (c == g * 2 + z - 14)
    elif kind == "y_lo":
        hit = (y < 2) & (c == b * 32 + y * 16 + z)
    else:
        hit = (y >= 14) & (c == b * 32 + (y - 14) * 16 + z)
    return jnp.where(hit, 1.0, 0.0).astype(BF16)


def _compress(cur, kind):
    lanes = cur.shape[1]
    return _exact_dot(cur, _select(kind, (lanes, 128), 0))


def _expand(h, kind, lanes):
    return _exact_dot(h, _select(kind, (128, lanes), 1))


def _emit_halos(cur, zlo_ref, zhi_ref, ylo_ref, yhi_ref):
    zlo_ref[...] = _compress(cur, "z_lo")
    zhi_ref[...] = _compress(cur, "z_hi")
    ylo_ref[...] = _compress(cur, "y_lo")
    yhi_ref[...] = _compress(cur, "y_hi")


def _emit_send(pick_ref, cur, snd_ref):
    snd_ref[...] = jnp.dot(
        pick_ref[...], cur.astype(BF16), preferred_element_type=F32
    ).astype(BF16)


def _prep_kernel(pick_ref, cur_ref, snd_ref, zlo_ref, zhi_ref, ylo_ref, yhi_ref):
    cur = cur_ref[...]
    _emit_send(pick_ref, cur, snd_ref)
    _emit_halos(cur, zlo_ref, zhi_ref, ylo_ref, yhi_ref)


def _halo_kernel(cur_ref, zlo_ref, zhi_ref, ylo_ref, yhi_ref):
    _emit_halos(cur_ref[...], zlo_ref, zhi_ref, ylo_ref, yhi_ref)


def _finish_kernel(last, pick_ref, sel_ref, inc_ref, p_ref, q_ref, w_ref, *refs):
    if last:
        cur_ref, g_scr, acc_scr = refs
    else:
        cur_ref, snd_ref, g_scr, acc_scr = refs
    t = pl.program_id(0)
    rows = p_ref.shape[0]

    @pl.when(t == 0)
    def _():
        summed = jnp.dot(sel_ref[...], inc_ref[...], preferred_element_type=F32)
        g_scr[...] = summed.astype(BF16)
        acc_scr[...] = jnp.zeros_like(acc_scr)

    grouped = g_scr[pl.ds(pl.multiple_of(t * rows, rows), rows), :]
    acc_scr[...] += lax.dot_general(
        grouped, w_ref[0], (((1,), (1,)), ((), ())), preferred_element_type=F32
    )

    @pl.when(t == pl.num_programs(0) - 1)
    def _():
        cur = (p_ref[...] + acc_scr[...]) - q_ref[...]
        cur_ref[...] = cur
        if not last:
            _emit_send(pick_ref, cur, snd_ref)


def _deriv(a1, m1, a2, m2):
    return (8.0 * (a1 - m1) - (a2 - m2)) / 12.0


def _drift_kernel(cur_ref, xlo_ref, xhi_ref, hyp_ref, hym_ref, hzp_ref, hzm_ref,
                  fx_ref, fy_ref, fz_ref, rate_ref, p_ref, q_ref, ext_ref):
    rows, lanes = cur_ref.shape
    cur = cur_ref[...]
    ext_ref[0:16, :] = xlo_ref[...]
    ext_ref[16:16 + rows, :] = cur
    ext_ref[16 + rows:32 + rows, :] = xhi_ref[...]
    dx = _deriv(ext_ref[24:24 + rows, :], ext_ref[8:8 + rows, :],
                ext_ref[32:32 + rows, :], ext_ref[0:rows, :])

    k = lax.broadcasted_iota(jnp.int32, (rows, lanes), 1)
    z = k & 15
    y = (k >> 4) & 15

    eyp = _expand(hyp_ref[...], "y_hi", lanes)
    eym = _expand(hym_ref[...], "y_lo", lanes)
    yp1 = jnp.where(y == 15, pltpu.roll(eyp, 16, 1), pltpu.roll(cur, lanes - 16, 1))
    yp2 = jnp.where(y >= 14, eyp, pltpu.roll(cur, lanes - 32, 1))
    ym1 = jnp.where(y == 0, pltpu.roll(eym, lanes - 16, 1), pltpu.roll(cur, 16, 1))
    ym2 = jnp.where(y <= 1, eym, pltpu.roll(cur, 32, 1))
    dy = _deriv(yp1, ym1, yp2, ym2)

    ezp = _expand(hzp_ref[...], "z_hi", lanes)
    ezm = _expand(hzm_ref[...], "z_lo", lanes)
    zp1 = jnp.where(z == 15, pltpu.roll(ezp, 1, 1), pltpu.roll(cur, lanes - 1, 1))
    zp2 = jnp.where(z >= 14, ezp, pltpu.roll(cur, lanes - 2, 1))
    zm1 = jnp.where(z == 0, pltpu.roll(ezm, lanes - 1, 1), pltpu.roll(cur, 1, 1))
    zm2 = jnp.where(z <= 1, ezm, pltpu.roll(cur, 2, 1))
    dz = _deriv(zp1, zm1, zp2, zm2)

    drift = fx_ref[...] * dx
    drift = drift + fy_ref[...] * dy
    drift = drift + fz_ref[...] * dz
    p_ref[...] = cur - drift
    q_ref[...] = rate_ref[...] * cur


def _full(shape):
    zeros = (0,) * len(shape)
    return pl.BlockSpec(shape, lambda *_: zeros)


def _send_shape(lanes, peers, both):
    return jax.ShapeDtypeStruct((peers * both, lanes), BF16)


def _prep(pick, cur, peers, both):
    halo = jax.ShapeDtypeStruct((cur.shape[0], 128), F32)
    shapes = [_send_shape(cur.shape[1], peers, both)] + [halo] * 4
    return pl.pallas_call(_prep_kernel, out_shape=shapes)(pick, cur)


def _halos(cur):
    halo = jax.ShapeDtypeStruct((cur.shape[0], 128), F32)
    return pl.pallas_call(_halo_kernel, out_shape=[halo] * 4)(cur)


def _finish(last, pick, sel, inc, p, q, tiles, peers, both):
    rows, lanes = p.shape
    tile_count = tiles.shape[0]
    shapes = [jax.ShapeDtypeStruct((rows, lanes), F32)]
    if not last:
        shapes.append(_send_shape(lanes, peers, both))
    outs = pl.pallas_call(
        functools.partial(_finish_kernel, last),
        out_shape=shapes,
        grid=(tile_count,),
        in_specs=[
            _full(pick.shape),
            _full(sel.shape),
            _full(inc.shape),
            _full(p.shape),
            _full(q.shape),
            pl.BlockSpec((1,) + tiles.shape[1:], lambda t: (t, 0, 0)),
        ],
        out_specs=[_full(x.shape) for x in shapes],
        scratch_shapes=[
            pltpu.VMEM((tile_count * rows, lanes), BF16),
            pltpu.VMEM((rows, lanes), F32),
        ],
        compiler_params=pltpu.CompilerParams(dimension_semantics=("arbitrary",)),
    )(pick, sel, inc, p, q, tiles)
    return outs[0], outs[1:]


def _drift(cur, xlo, xhi, hyp, hym, hzp, hzm, fx, fy, fz, rate):
    rows, lanes = cur.shape
    plane = jax.ShapeDtypeStruct((rows, lanes), F32)
    return pl.pallas_call(
        _drift_kernel,
        out_shape=[plane, plane],
        scratch_shapes=[pltpu.VMEM((rows + 32, lanes), F32)],
    )(cur, xlo, xhi, hyp, hym, hzp, hzm, fx, fy, fz, rate)


def _ring(axis):
    size = lax.axis_size(axis)
    up = [(i, (i + 1) % size) for i in range(size)]
    down = [(j, i) for i, j in up]
    return up, down


def per_device(populations, force, rate, tiles, send_planes, recv_target, recv_tile, recv_count):
    width_x, drive_count, band_count, width_y, width_z = populations.shape
    rows = width_x * drive_count
    lanes = band_count * width_y * width_z
    peer_count = lax.axis_size("kz")
    slot_cap = send_planes.shape[-1]
    tile_count = tiles.shape[0]
    plane_list = send_planes.reshape(peer_count * slot_cap)
    slot_count = recv_count.reshape(peer_count)
    target_ids = recv_target.reshape(peer_count, slot_cap)
    tile_ids = recv_tile.reshape(peer_count, slot_cap)
    usable = lax.broadcasted_iota(jnp.int32, (peer_count, slot_cap), 1) < slot_count[:, None]
    tile_match = (
        tile_ids[None, None] == jnp.arange(tile_count, dtype=jnp.int32)[:, None, None, None]
    )
    plane_match = (
        target_ids[None, None] == jnp.arange(width_x, dtype=jnp.int32)[None, :, None, None]
    )
    selector = (tile_match & plane_match & usable[None, None]).astype(BF16)
    flat_tile = jnp.repeat(tile_ids.reshape(-1), drive_count)
    flat_target = jnp.repeat(target_ids.reshape(-1), drive_count)
    flat_usable = jnp.repeat(usable.reshape(-1), drive_count)
    big_rows = tile_count * width_x * drive_count
    big_cols = peer_count * slot_cap * drive_count
    r = lax.broadcasted_iota(jnp.int32, (big_rows, big_cols), 0)
    col = lax.broadcasted_iota(jnp.int32, (big_rows, big_cols), 1)
    hit = (r // (width_x * drive_count)) == flat_tile[None, :]
    hit = hit & (((r // drive_count) % width_x) == flat_target[None, :])
    hit = hit & flat_usable[None, :] & ((r % drive_count) == (col % drive_count))
    sel_big = hit.astype(BF16)
    both = slot_cap * drive_count
    flat_plane = jnp.repeat(plane_list, drive_count)
    pr = lax.broadcasted_iota(jnp.int32, (peer_count * both, rows), 0)
    pc = lax.broadcasted_iota(jnp.int32, (peer_count * both, rows), 1)
    pick = ((flat_plane[:, None] == pc // drive_count) & (pr % drive_count == pc % drive_count)).astype(BF16)

    def spread(a):
        a = a.reshape(width_x, 1, lanes)
        return jnp.broadcast_to(a, (width_x, drive_count, lanes)).reshape(rows, lanes)

    fx = spread(force[:, 0])
    fy = spread(force[:, 1])
    fz = spread(force[:, 2])
    rate_wide = spread(rate)

    up_x, down_x = _ring("kx")
    up_y, down_y = _ring("ky")
    up_z, down_z = _ring("kz")

    cur = populations.reshape(rows, lanes)
    snd, zlo, zhi, ylo, yhi = _prep(pick, cur, peer_count, both)
    for iteration in range(ITERS):
        last = iteration + 1 == ITERS
        if iteration > 0:
            zlo, zhi, ylo, yhi = _halos(cur)
        xlo = lax.ppermute(cur[rows - 16:], "kx", up_x)
        xhi = lax.ppermute(cur[:16], "kx", down_x)
        hym = lax.ppermute(yhi, "ky", up_y)
        hyp = lax.ppermute(ylo, "ky", down_y)
        hzm = lax.ppermute(zhi, "kz", up_z)
        hzp = lax.ppermute(zlo, "kz", down_z)
        outgoing = snd.reshape(peer_count, both, lanes)
        incoming = lax.all_to_all(outgoing, "kz", split_axis=0, concat_axis=0, tiled=True)
        p, q = _drift(cur, xlo, xhi, hyp, hym, hzp, hzm, fx, fy, fz, rate_wide)
        inc = incoming.reshape(peer_count * both, lanes)
        cur, rest = _finish(last, pick, sel_big, inc, p, q, tiles, peer_count, both)
        if not last:
            (snd,) = rest
    return cur.reshape(width_x, drive_count, band_count, width_y, width_z)


def solution(mesh):
    placed = (
        P("kx", None, None, "ky", "kz"),
        P("kx", None, None, "ky", "kz"),
        P("kx", None, "ky", "kz"),
        P(),
        P("kx", "ky", "kz", None, None),
        P("kx", "ky", "kz", None, None),
        P("kx", "ky", "kz", None, None),
        P("kx", "ky", "kz", None),
    )
    return jax.shard_map(
        per_device,
        mesh=mesh,
        in_specs=placed,
        out_specs=P("kx", None, None, "ky", "kz"),
        check_vma=False,
    )
```

```python
import functools

import jax
import jax.numpy as jnp
from jax import lax
from jax.experimental import pallas as pl
from jax.experimental.pallas import tpu as pltpu
from jax.sharding import PartitionSpec as P

ITERS = 2
F32 = jnp.float32
BF16 = jnp.bfloat16


def _split3(h):
    hi = h.astype(BF16)
    rest = h - hi.astype(F32)
    mid = rest.astype(BF16)
    lo = (rest - mid.astype(F32)).astype(BF16)
    return hi, mid, lo


def _exact_dot(h, m):
    hi, mid, lo = _split3(h)
    out = jnp.dot(hi, m, preferred_element_type=F32)
    out = out + jnp.dot(mid, m, preferred_element_type=F32)
    return out + jnp.dot(lo, m, preferred_element_type=F32)


def _select(kind, shape, k_axis):
    k = lax.broadcasted_iota(jnp.int32, shape, k_axis)
    c = lax.broadcasted_iota(jnp.int32, shape, 1 - k_axis)
    z = k & 15
    y = (k >> 4) & 15
    g = k >> 4
    b = k >> 8
    if kind == "z_lo":
        hit = (z < 2) & (c == g * 2 + z)
    elif kind == "z_hi":
        hit = (z >= 14) & (c == g * 2 + z - 14)
    elif kind == "y_lo":
        hit = (y < 2) & (c == b * 32 + y * 16 + z)
    else:
        hit = (y >= 14) & (c == b * 32 + (y - 14) * 16 + z)
    return jnp.where(hit, 1.0, 0.0).astype(BF16)


def _compress(cur, kind):
    lanes = cur.shape[1]
    return _exact_dot(cur, _select(kind, (lanes, 128), 0))


def _expand(h, kind, lanes):
    return _exact_dot(h, _select(kind, (128, lanes), 1))


def _emit_halos(cur, zlo_ref, zhi_ref, ylo_ref, yhi_ref):
    zlo_ref[...] = _compress(cur, "z_lo")
    zhi_ref[...] = _compress(cur, "z_hi")
    ylo_ref[...] = _compress(cur, "y_lo")
    yhi_ref[...] = _compress(cur, "y_hi")


def _emit_send(pick_ref, cur, snd_ref):
    snd_ref[...] = jnp.dot(
        pick_ref[...], cur.astype(BF16), preferred_element_type=F32
    ).astype(BF16)


def _prep_kernel(pick_ref, cur_ref, snd_ref, zlo_ref, zhi_ref, ylo_ref, yhi_ref):
    cur = cur_ref[...]
    _emit_send(pick_ref, cur, snd_ref)
    _emit_halos(cur, zlo_ref, zhi_ref, ylo_ref, yhi_ref)


def _halo_kernel(cur_ref, zlo_ref, zhi_ref, ylo_ref, yhi_ref):
    _emit_halos(cur_ref[...], zlo_ref, zhi_ref, ylo_ref, yhi_ref)


def _finish_kernel(last, pick_ref, sel_ref, inc_ref, cur_ref, a_ref, q_ref, fz_ref,
                   hzp_ref, hzm_ref, w_ref, *refs):
    if last:
        out_ref, g_scr, acc_scr, p_scr = refs
    else:
        out_ref, snd_ref, g_scr, acc_scr, p_scr = refs
    t = pl.program_id(0)
    rows, _ = cur_ref.shape

    @pl.when(t == 0)
    def _():
        summed = jnp.dot(sel_ref[...], inc_ref[...], preferred_element_type=F32)
        g_scr[...] = summed.astype(BF16)
        acc_scr[...] = jnp.zeros_like(acc_scr)
        cur = cur_ref[...]
        dz = _deriv_z(cur, hzp_ref[...], hzm_ref[...])
        drift = a_ref[...] + fz_ref[...] * dz
        p_scr[...] = cur - drift

    grouped = g_scr[pl.ds(pl.multiple_of(t * rows, rows), rows), :]
    acc_scr[...] += lax.dot_general(
        grouped, w_ref[0], (((1,), (1,)), ((), ())), preferred_element_type=F32
    )

    @pl.when(t == pl.num_programs(0) - 1)
    def _():
        cur = (p_scr[...] + acc_scr[...]) - q_ref[...]
        out_ref[...] = cur
        if not last:
            _emit_send(pick_ref, cur, snd_ref)


def _deriv(a1, m1, a2, m2):
    return (8.0 * (a1 - m1) - (a2 - m2)) / 12.0


def _deriv_z(cur, hzp, hzm):
    rows, lanes = cur.shape
    z = lax.broadcasted_iota(jnp.int32, (rows, lanes), 1) & 15
    ezp = _expand(hzp, "z_hi", lanes)
    ezm = _expand(hzm, "z_lo", lanes)
    zp1 = jnp.where(z == 15, pltpu.roll(ezp, 1, 1), pltpu.roll(cur, lanes - 1, 1))
    zp2 = jnp.where(z >= 14, ezp, pltpu.roll(cur, lanes - 2, 1))
    zm1 = jnp.where(z == 0, pltpu.roll(ezm, lanes - 1, 1), pltpu.roll(cur, 1, 1))
    zm2 = jnp.where(z <= 1, ezm, pltpu.roll(cur, 2, 1))
    return _deriv(zp1, zm1, zp2, zm2)


def _drift_kernel(cur_ref, xlo_ref, xhi_ref, hyp_ref, hym_ref,
                  fx_ref, fy_ref, rate_ref, a_ref, q_ref, ext_ref):
    rows, lanes = cur_ref.shape
    cur = cur_ref[...]
    ext_ref[0:16, :] = xlo_ref[...]
    ext_ref[16:16 + rows, :] = cur
    ext_ref[16 + rows:32 + rows, :] = xhi_ref[...]
    dx = _deriv(ext_ref[24:24 + rows, :], ext_ref[8:8 + rows, :],
                ext_ref[32:32 + rows, :], ext_ref[0:rows, :])

    k = lax.broadcasted_iota(jnp.int32, (rows, lanes), 1)
    y = (k >> 4) & 15
    eyp = _expand(hyp_ref[...], "y_hi", lanes)
    eym = _expand(hym_ref[...], "y_lo", lanes)
    yp1 = jnp.where(y == 15, pltpu.roll(eyp, 16, 1), pltpu.roll(cur, lanes - 16, 1))
    yp2 = jnp.where(y >= 14, eyp, pltpu.roll(cur, lanes - 32, 1))
    ym1 = jnp.where(y == 0, pltpu.roll(eym, lanes - 16, 1), pltpu.roll(cur, 16, 1))
    ym2 = jnp.where(y <= 1, eym, pltpu.roll(cur, 32, 1))
    dy = _deriv(yp1, ym1, yp2, ym2)

    drift = fx_ref[...] * dx
    a_ref[...] = drift + fy_ref[...] * dy
    q_ref[...] = rate_ref[...] * cur


def _full(shape):
    zeros = (0,) * len(shape)
    return pl.BlockSpec(shape, lambda *_: zeros)


def _send_shape(lanes, peers, both):
    return jax.ShapeDtypeStruct((peers * both, lanes), BF16)


def _prep(pick, cur, peers, both):
    halo = jax.ShapeDtypeStruct((cur.shape[0], 128), F32)
    shapes = [_send_shape(cur.shape[1], peers, both)] + [halo] * 4
    return pl.pallas_call(_prep_kernel, out_shape=shapes)(pick, cur)


def _halos(cur):
    halo = jax.ShapeDtypeStruct((cur.shape[0], 128), F32)
    return pl.pallas_call(_halo_kernel, out_shape=[halo] * 4)(cur)


def _finish(last, pick, sel, inc, cur, a, q, fz, hzp, hzm, tiles, peers, both):
    rows, lanes = cur.shape
    tile_count = tiles.shape[0]
    shapes = [jax.ShapeDtypeStruct((rows, lanes), F32)]
    if not last:
        shapes.append(_send_shape(lanes, peers, both))
    small = (pick, sel, inc, cur, a, q, fz, hzp, hzm)
    outs = pl.pallas_call(
        functools.partial(_finish_kernel, last),
        out_shape=shapes,
        grid=(tile_count,),
        in_specs=[_full(x.shape) for x in small]
        + [pl.BlockSpec((1,) + tiles.shape[1:], lambda t: (t, 0, 0))],
        out_specs=[_full(x.shape) for x in shapes],
        scratch_shapes=[
            pltpu.VMEM((tile_count * rows, lanes), BF16),
            pltpu.VMEM((rows, lanes), F32),
            pltpu.VMEM((rows, lanes), F32),
        ],
        compiler_params=pltpu.CompilerParams(dimension_semantics=("arbitrary",)),
    )(*small, tiles)
    return outs[0], outs[1:]


def _drift(cur, xlo, xhi, hyp, hym, fx, fy, rate):
    rows, lanes = cur.shape
    plane = jax.ShapeDtypeStruct((rows, lanes), F32)
    return pl.pallas_call(
        _drift_kernel,
        out_shape=[plane, plane],
        scratch_shapes=[pltpu.VMEM((rows + 32, lanes), F32)],
    )(cur, xlo, xhi, hyp, hym, fx, fy, rate)


def _ring(axis):
    size = lax.axis_size(axis)
    up = [(i, (i + 1) % size) for i in range(size)]
    down = [(j, i) for i, j in up]
    return up, down


def per_device(populations, force, rate, tiles, send_planes, recv_target, recv_tile, recv_count):
    width_x, drive_count, band_count, width_y, width_z = populations.shape
    rows = width_x * drive_count
    lanes = band_count * width_y * width_z
    peer_count = lax.axis_size("kz")
    slot_cap = send_planes.shape[-1]
    tile_count = tiles.shape[0]
    plane_list = send_planes.reshape(peer_count * slot_cap)
    slot_count = recv_count.reshape(peer_count)
    target_ids = recv_target.reshape(peer_count, slot_cap)
    tile_ids = recv_tile.reshape(peer_count, slot_cap)
    usable = lax.broadcasted_iota(jnp.int32, (peer_count, slot_cap), 1) < slot_count[:, None]
    tile_match = (
        tile_ids[None, None] == jnp.arange(tile_count, dtype=jnp.int32)[:, None, None, None]
    )
    plane_match = (
        target_ids[None, None] == jnp.arange(width_x, dtype=jnp.int32)[None, :, None, None]
    )
    selector = (tile_match & plane_match & usable[None, None]).astype(BF16)
    flat_tile = jnp.repeat(tile_ids.reshape(-1), drive_count)
    flat_target = jnp.repeat(target_ids.reshape(-1), drive_count)
    flat_usable = jnp.repeat(usable.reshape(-1), drive_count)
    big_rows = tile_count * width_x * drive_count
    big_cols = peer_count * slot_cap * drive_count
    r = lax.broadcasted_iota(jnp.int32, (big_rows, big_cols), 0)
    col = lax.broadcasted_iota(jnp.int32, (big_rows, big_cols), 1)
    hit = (r // (width_x * drive_count)) == flat_tile[None, :]
    hit = hit & (((r // drive_count) % width_x) == flat_target[None, :])
    hit = hit & flat_usable[None, :] & ((r % drive_count) == (col % drive_count))
    sel_big = hit.astype(BF16)
    both = slot_cap * drive_count
    flat_plane = jnp.repeat(plane_list, drive_count)
    pr = lax.broadcasted_iota(jnp.int32, (peer_count * both, rows), 0)
    pc = lax.broadcasted_iota(jnp.int32, (peer_count * both, rows), 1)
    pick = ((flat_plane[:, None] == pc // drive_count) & (pr % drive_count == pc % drive_count)).astype(BF16)

    def spread(a):
        a = a.reshape(width_x, 1, lanes)
        return jnp.broadcast_to(a, (width_x, drive_count, lanes)).reshape(rows, lanes)

    fx = spread(force[:, 0])
    fy = spread(force[:, 1])
    fz = spread(force[:, 2])
    rate_wide = spread(rate)

    up_x, down_x = _ring("kx")
    up_y, down_y = _ring("ky")
    up_z, down_z = _ring("kz")

    cur = populations.reshape(rows, lanes)
    snd, zlo, zhi, ylo, yhi = _prep(pick, cur, peer_count, both)
    for iteration in range(ITERS):
        last = iteration + 1 == ITERS
        if iteration > 0:
            zlo, zhi, ylo, yhi = _halos(cur)
        xlo = lax.ppermute(cur[rows - 16:], "kx", up_x)
        xhi = lax.ppermute(cur[:16], "kx", down_x)
        hym = lax.ppermute(yhi, "ky", up_y)
        hyp = lax.ppermute(ylo, "ky", down_y)
        hzm = lax.ppermute(zhi, "kz", up_z)
        hzp = lax.ppermute(zlo, "kz", down_z)
        outgoing = snd.reshape(peer_count, both, lanes)
        incoming = lax.all_to_all(outgoing, "kz", split_axis=0, concat_axis=0, tiled=True)
        a, q = _drift(cur, xlo, xhi, hyp, hym, fx, fy, rate_wide)
        inc = incoming.reshape(peer_count * both, lanes)
        cur, rest = _finish(
            last, pick, sel_big, inc, cur, a, q, fz, hzp, hzm, tiles, peer_count, both
        )
        if not last:
            (snd,) = rest
    return cur.reshape(width_x, drive_count, band_count, width_y, width_z)


def solution(mesh):
    placed = (
        P("kx", None, None, "ky", "kz"),
        P("kx", None, None, "ky", "kz"),
        P("kx", None, "ky", "kz"),
        P(),
        P("kx", "ky", "kz", None, None),
        P("kx", "ky", "kz", None, None),
        P("kx", "ky", "kz", None, None),
        P("kx", "ky", "kz", None),
    )
    return jax.shard_map(
        per_device,
        mesh=mesh,
        in_specs=placed,
        out_specs=P("kx", None, None, "ky", "kz"),
        check_vma=False,
    )
```

```python
import functools

import jax
import jax.numpy as jnp
from jax import lax
from jax.experimental import pallas as pl
from jax.experimental.pallas import tpu as pltpu
from jax.sharding import PartitionSpec as P

ITERS = 2
F32 = jnp.float32
BF16 = jnp.bfloat16


def _split3(h):
    hi = h.astype(BF16)
    rest = h - hi.astype(F32)
    mid = rest.astype(BF16)
    lo = (rest - mid.astype(F32)).astype(BF16)
    return hi, mid, lo


def _exact_dot(h, m):
    hi, mid, lo = _split3(h)
    out = jnp.dot(hi, m, preferred_element_type=F32)
    out = out + jnp.dot(mid, m, preferred_element_type=F32)
    return out + jnp.dot(lo, m, preferred_element_type=F32)


def _select(kind, shape, k_axis):
    k = lax.broadcasted_iota(jnp.int32, shape, k_axis)
    c = lax.broadcasted_iota(jnp.int32, shape, 1 - k_axis)
    z = k & 15
    y = (k >> 4) & 15
    g = k >> 4
    b = k >> 8
    if kind == "z_lo":
        hit = (z < 2) & (c == g * 2 + z)
    elif kind == "z_hi":
        hit = (z >= 14) & (c == g * 2 + z - 14)
    elif kind == "y_lo":
        hit = (y < 2) & (c == b * 32 + y * 16 + z)
    else:
        hit = (y >= 14) & (c == b * 32 + (y - 14) * 16 + z)
    return jnp.where(hit, 1.0, 0.0).astype(BF16)


def _compress(cur, kind):
    lanes = cur.shape[1]
    return _exact_dot(cur, _select(kind, (lanes, 128), 0))


def _expand(h, kind, lanes):
    return _exact_dot(h, _select(kind, (128, lanes), 1))


def _emit_halos(cur, zlo_ref, zhi_ref, ylo_ref, yhi_ref):
    zlo_ref[...] = _compress(cur, "z_lo")
    zhi_ref[...] = _compress(cur, "z_hi")
    ylo_ref[...] = _compress(cur, "y_lo")
    yhi_ref[...] = _compress(cur, "y_hi")


def _emit_send(pick_ref, cur, snd_ref):
    snd_ref[...] = jnp.dot(
        pick_ref[...], cur.astype(BF16), preferred_element_type=F32
    ).astype(BF16)


def _prep_kernel(pick_ref, cur_ref, snd_ref, zlo_ref, zhi_ref, ylo_ref, yhi_ref):
    cur = cur_ref[...]
    _emit_send(pick_ref, cur, snd_ref)
    _emit_halos(cur, zlo_ref, zhi_ref, ylo_ref, yhi_ref)


def _halo_kernel(cur_ref, zlo_ref, zhi_ref, ylo_ref, yhi_ref):
    _emit_halos(cur_ref[...], zlo_ref, zhi_ref, ylo_ref, yhi_ref)


def _finish_kernel(last, pick_ref, sel_ref, inc_ref, cur_ref, a_ref, q_ref, fz_ref,
                   hzp_ref, hzm_ref, w_hbm, *refs):
    if last:
        out_ref, w_buf, sems = refs
    else:
        out_ref, snd_ref, w_buf, sems = refs
    rows = cur_ref.shape[0]
    tile_count = w_hbm.shape[0]
    copies = [
        pltpu.make_async_copy(w_hbm.at[t], w_buf.at[t], sems.at[t]) for t in range(tile_count)
    ]
    for copy in copies:
        copy.start()
    grouped = jnp.dot(sel_ref[...], inc_ref[...], preferred_element_type=F32).astype(BF16)
    cur = cur_ref[...]
    dz = _deriv_z(cur, hzp_ref[...], hzm_ref[...])
    drift = a_ref[...] + fz_ref[...] * dz
    p = cur - drift
    coll = None
    for t in range(tile_count):
        copies[t].wait()
        part = lax.dot_general(
            grouped[t * rows:(t + 1) * rows], w_buf[t], (((1,), (1,)), ((), ())),
            preferred_element_type=F32,
        )
        coll = part if coll is None else coll + part
    cur = (p + coll) - q_ref[...]
    out_ref[...] = cur
    if not last:
        _emit_send(pick_ref, cur, snd_ref)


def _deriv(a1, m1, a2, m2):
    return (8.0 * (a1 - m1) - (a2 - m2)) / 12.0


def _deriv_z(cur, hzp, hzm):
    rows, lanes = cur.shape
    z = lax.broadcasted_iota(jnp.int32, (rows, lanes), 1) & 15
    ezp = _expand(hzp, "z_hi", lanes)
    ezm = _expand(hzm, "z_lo", lanes)
    zp1 = jnp.where(z == 15, pltpu.roll(ezp, 1, 1), pltpu.roll(cur, lanes - 1, 1))
    zp2 = jnp.where(z >= 14, ezp, pltpu.roll(cur, lanes - 2, 1))
    zm1 = jnp.where(z == 0, pltpu.roll(ezm, lanes - 1, 1), pltpu.roll(cur, 1, 1))
    zm2 = jnp.where(z <= 1, ezm, pltpu.roll(cur, 2, 1))
    return _deriv(zp1, zm1, zp2, zm2)


def _drift_kernel(cur_ref, xlo_ref, xhi_ref, hyp_ref, hym_ref,
                  fx_ref, fy_ref, rate_ref, a_ref, q_ref, ext_ref):
    rows, lanes = cur_ref.shape
    cur = cur_ref[...]
    ext_ref[0:16, :] = xlo_ref[...]
    ext_ref[16:16 + rows, :] = cur
    ext_ref[16 + rows:32 + rows, :] = xhi_ref[...]
    dx = _deriv(ext_ref[24:24 + rows, :], ext_ref[8:8 + rows, :],
                ext_ref[32:32 + rows, :], ext_ref[0:rows, :])

    k = lax.broadcasted_iota(jnp.int32, (rows, lanes), 1)
    y = (k >> 4) & 15
    eyp = _expand(hyp_ref[...], "y_hi", lanes)
    eym = _expand(hym_ref[...], "y_lo", lanes)
    yp1 = jnp.where(y == 15, pltpu.roll(eyp, 16, 1), pltpu.roll(cur, lanes - 16, 1))
    yp2 = jnp.where(y >= 14, eyp, pltpu.roll(cur, lanes - 32, 1))
    ym1 = jnp.where(y == 0, pltpu.roll(eym, lanes - 16, 1), pltpu.roll(cur, 16, 1))
    ym2 = jnp.where(y <= 1, eym, pltpu.roll(cur, 32, 1))
    dy = _deriv(yp1, ym1, yp2, ym2)

    drift = fx_ref[...] * dx
    a_ref[...] = drift + fy_ref[...] * dy
    q_ref[...] = rate_ref[...] * cur


def _send_shape(lanes, peers, both):
    return jax.ShapeDtypeStruct((peers * both, lanes), BF16)


def _prep(pick, cur, peers, both):
    halo = jax.ShapeDtypeStruct((cur.shape[0], 128), F32)
    shapes = [_send_shape(cur.shape[1], peers, both)] + [halo] * 4
    return pl.pallas_call(_prep_kernel, out_shape=shapes)(pick, cur)


def _halos(cur):
    halo = jax.ShapeDtypeStruct((cur.shape[0], 128), F32)
    return pl.pallas_call(_halo_kernel, out_shape=[halo] * 4)(cur)


def _finish(last, pick, sel, inc, cur, a, q, fz, hzp, hzm, tiles, peers, both):
    rows, lanes = cur.shape
    shapes = [jax.ShapeDtypeStruct((rows, lanes), F32)]
    if not last:
        shapes.append(_send_shape(lanes, peers, both))
    small = (pick, sel, inc, cur, a, q, fz, hzp, hzm)
    vmem = pl.BlockSpec(memory_space=pltpu.VMEM)
    outs = pl.pallas_call(
        functools.partial(_finish_kernel, last),
        out_shape=shapes,
        in_specs=[vmem] * len(small) + [pl.BlockSpec(memory_space=pl.ANY)],
        out_specs=[vmem] * len(shapes),
        scratch_shapes=[
            pltpu.VMEM(tiles.shape, tiles.dtype),
            pltpu.SemaphoreType.DMA((tiles.shape[0],)),
        ],
        compiler_params=pltpu.CompilerParams(vmem_limit_bytes=40 * 1024 * 1024),
    )(*small, tiles)
    return outs[0], outs[1:]


def _drift(cur, xlo, xhi, hyp, hym, fx, fy, rate):
    rows, lanes = cur.shape
    plane = jax.ShapeDtypeStruct((rows, lanes), F32)
    return pl.pallas_call(
        _drift_kernel,
        out_shape=[plane, plane],
        scratch_shapes=[pltpu.VMEM((rows + 32, lanes), F32)],
    )(cur, xlo, xhi, hyp, hym, fx, fy, rate)


def _ring(axis):
    size = lax.axis_size(axis)
    up = [(i, (i + 1) % size) for i in range(size)]
    down = [(j, i) for i, j in up]
    return up, down


def per_device(populations, force, rate, tiles, send_planes, recv_target, recv_tile, recv_count):
    width_x, drive_count, band_count, width_y, width_z = populations.shape
    rows = width_x * drive_count
    lanes = band_count * width_y * width_z
    peer_count = lax.axis_size("kz")
    slot_cap = send_planes.shape[-1]
    tile_count = tiles.shape[0]
    plane_list = send_planes.reshape(peer_count * slot_cap)
    slot_count = recv_count.reshape(peer_count)
    target_ids = recv_target.reshape(peer_count, slot_cap)
    tile_ids = recv_tile.reshape(peer_count, slot_cap)
    usable = lax.broadcasted_iota(jnp.int32, (peer_count, slot_cap), 1) < slot_count[:, None]
    tile_match = (
        tile_ids[None, None] == jnp.arange(tile_count, dtype=jnp.int32)[:, None, None, None]
    )
    plane_match = (
        target_ids[None, None] == jnp.arange(width_x, dtype=jnp.int32)[None, :, None, None]
    )
    selector = (tile_match & plane_match & usable[None, None]).astype(BF16)
    flat_tile = jnp.repeat(tile_ids.reshape(-1), drive_count)
    flat_target = jnp.repeat(target_ids.reshape(-1), drive_count)
    flat_usable = jnp.repeat(usable.reshape(-1), drive_count)
    big_rows = tile_count * width_x * drive_count
    big_cols = peer_count * slot_cap * drive_count
    r = lax.broadcasted_iota(jnp.int32, (big_rows, big_cols), 0)
    col = lax.broadcasted_iota(jnp.int32, (big_rows, big_cols), 1)
    hit = (r // (width_x * drive_count)) == flat_tile[None, :]
    hit = hit & (((r // drive_count) % width_x) == flat_target[None, :])
    hit = hit & flat_usable[None, :] & ((r % drive_count) == (col % drive_count))
    sel_big = hit.astype(BF16)
    both = slot_cap * drive_count
    flat_plane = jnp.repeat(plane_list, drive_count)
    pr = lax.broadcasted_iota(jnp.int32, (peer_count * both, rows), 0)
    pc = lax.broadcasted_iota(jnp.int32, (peer_count * both, rows), 1)
    pick = ((flat_plane[:, None] == pc // drive_count) & (pr % drive_count == pc % drive_count)).astype(BF16)

    def spread(a):
        a = a.reshape(width_x, 1, lanes)
        return jnp.broadcast_to(a, (width_x, drive_count, lanes)).reshape(rows, lanes)

    fx = spread(force[:, 0])
    fy = spread(force[:, 1])
    fz = spread(force[:, 2])
    rate_wide = spread(rate)

    up_x, down_x = _ring("kx")
    up_y, down_y = _ring("ky")
    up_z, down_z = _ring("kz")

    cur = populations.reshape(rows, lanes)
    snd, zlo, zhi, ylo, yhi = _prep(pick, cur, peer_count, both)
    for iteration in range(ITERS):
        last = iteration + 1 == ITERS
        if iteration > 0:
            zlo, zhi, ylo, yhi = _halos(cur)
        xlo = lax.ppermute(cur[rows - 16:], "kx", up_x)
        xhi = lax.ppermute(cur[:16], "kx", down_x)
        hym = lax.ppermute(yhi, "ky", up_y)
        hyp = lax.ppermute(ylo, "ky", down_y)
        hzm = lax.ppermute(zhi, "kz", up_z)
        hzp = lax.ppermute(zlo, "kz", down_z)
        outgoing = snd.reshape(peer_count, both, lanes)
        incoming = lax.all_to_all(outgoing, "kz", split_axis=0, concat_axis=0, tiled=True)
        a, q = _drift(cur, xlo, xhi, hyp, hym, fx, fy, rate_wide)
        inc = incoming.reshape(peer_count * both, lanes)
        cur, rest = _finish(
            last, pick, sel_big, inc, cur, a, q, fz, hzp, hzm, tiles, peer_count, both
        )
        if not last:
            (snd,) = rest
    return cur.reshape(width_x, drive_count, band_count, width_y, width_z)


def solution(mesh):
    placed = (
        P("kx", None, None, "ky", "kz"),
        P("kx", None, None, "ky", "kz"),
        P("kx", None, "ky", "kz"),
        P(),
        P("kx", "ky", "kz", None, None),
        P("kx", "ky", "kz", None, None),
        P("kx", "ky", "kz", None, None),
        P("kx", "ky", "kz", None),
    )
    return jax.shard_map(
        per_device,
        mesh=mesh,
        in_specs=placed,
        out_specs=P("kx", None, None, "ky", "kz"),
        check_vma=False,
    )
```

```python
import functools

import jax
import jax.numpy as jnp
from jax import lax
from jax.experimental import pallas as pl
from jax.experimental.pallas import tpu as pltpu
from jax.sharding import PartitionSpec as P

ITERS = 2
F32 = jnp.float32
BF16 = jnp.bfloat16


def _split3(h):
    hi = h.astype(BF16)
    rest = h - hi.astype(F32)
    mid = rest.astype(BF16)
    lo = (rest - mid.astype(F32)).astype(BF16)
    return hi, mid, lo


def _exact_dot(h, m):
    hi, mid, lo = _split3(h)
    out = jnp.dot(hi, m, preferred_element_type=F32)
    out = out + jnp.dot(mid, m, preferred_element_type=F32)
    return out + jnp.dot(lo, m, preferred_element_type=F32)


def _select(kind, shape, k_axis):
    k = lax.broadcasted_iota(jnp.int32, shape, k_axis)
    c = lax.broadcasted_iota(jnp.int32, shape, 1 - k_axis)
    z = k & 15
    y = (k >> 4) & 15
    g = k >> 4
    b = k >> 8
    if kind == "z_lo":
        hit = (z < 2) & (c == g * 2 + z)
    elif kind == "z_hi":
        hit = (z >= 14) & (c == g * 2 + z - 14)
    elif kind == "y_lo":
        hit = (y < 2) & (c == b * 32 + y * 16 + z)
    else:
        hit = (y >= 14) & (c == b * 32 + (y - 14) * 16 + z)
    return jnp.where(hit, 1.0, 0.0).astype(BF16)


def _compress(cur, kind):
    lanes = cur.shape[1]
    return _exact_dot(cur, _select(kind, (lanes, 128), 0))


def _expand(h, kind, lanes):
    return _exact_dot(h, _select(kind, (128, lanes), 1))


def _emit_halos(cur, zlo_ref, zhi_ref, ylo_ref, yhi_ref):
    zlo_ref[...] = _compress(cur, "z_lo")
    zhi_ref[...] = _compress(cur, "z_hi")
    ylo_ref[...] = _compress(cur, "y_lo")
    yhi_ref[...] = _compress(cur, "y_hi")


def _emit_send(pick_ref, cur, snd_ref):
    snd_ref[...] = jnp.dot(
        pick_ref[...], cur.astype(BF16), preferred_element_type=F32
    ).astype(BF16)


def _send_kernel(pick_ref, rnd_ref, snd_ref):
    snd_ref[...] = jnp.dot(
        pick_ref[...], rnd_ref[...], preferred_element_type=F32
    ).astype(BF16)


def _halo_kernel(cur_ref, zlo_ref, zhi_ref, ylo_ref, yhi_ref):
    _emit_halos(cur_ref[...], zlo_ref, zhi_ref, ylo_ref, yhi_ref)


def _finish_kernel(last, pick_ref, sel_ref, inc_ref, cur_ref, a_ref, q_ref, fz_ref,
                   hzp_ref, hzm_ref, w_ref, *refs):
    if last:
        out_ref, g_scr, acc_scr, p_scr = refs
    else:
        out_ref, snd_ref, g_scr, acc_scr, p_scr = refs
    t = pl.program_id(0)
    rows, _ = cur_ref.shape

    @pl.when(t == 0)
    def _():
        summed = jnp.dot(sel_ref[...], inc_ref[...], preferred_element_type=F32)
        g_scr[...] = summed.astype(BF16)
        acc_scr[...] = jnp.zeros_like(acc_scr)
        cur = cur_ref[...]
        dz = _deriv_z(cur, hzp_ref[...], hzm_ref[...])
        drift = a_ref[...] + fz_ref[...] * dz
        p_scr[...] = cur - drift

    grouped = g_scr[pl.ds(pl.multiple_of(t * rows, rows), rows), :]
    acc_scr[...] += lax.dot_general(
        grouped, w_ref[0], (((1,), (1,)), ((), ())), preferred_element_type=F32
    )

    @pl.when(t == pl.num_programs(0) - 1)
    def _():
        cur = (p_scr[...] + acc_scr[...]) - q_ref[...]
        out_ref[...] = cur
        if not last:
            _emit_send(pick_ref, cur, snd_ref)


def _deriv(a1, m1, a2, m2):
    return (8.0 * (a1 - m1) - (a2 - m2)) / 12.0


def _deriv_z(cur, hzp, hzm):
    rows, lanes = cur.shape
    z = lax.broadcasted_iota(jnp.int32, (rows, lanes), 1) & 15
    ezp = _expand(hzp, "z_hi", lanes)
    ezm = _expand(hzm, "z_lo", lanes)
    zp1 = jnp.where(z == 15, pltpu.roll(ezp, 1, 1), pltpu.roll(cur, lanes - 1, 1))
    zp2 = jnp.where(z >= 14, ezp, pltpu.roll(cur, lanes - 2, 1))
    zm1 = jnp.where(z == 0, pltpu.roll(ezm, lanes - 1, 1), pltpu.roll(cur, 1, 1))
    zm2 = jnp.where(z <= 1, ezm, pltpu.roll(cur, 2, 1))
    return _deriv(zp1, zm1, zp2, zm2)


def _drift_kernel(cur_ref, xlo_ref, xhi_ref, hyp_ref, hym_ref,
                  fx_ref, fy_ref, rate_ref, a_ref, q_ref, ext_ref):
    rows, lanes = cur_ref.shape
    cur = cur_ref[...]
    ext_ref[0:16, :] = xlo_ref[...]
    ext_ref[16:16 + rows, :] = cur
    ext_ref[16 + rows:32 + rows, :] = xhi_ref[...]
    dx = _deriv(ext_ref[24:24 + rows, :], ext_ref[8:8 + rows, :],
                ext_ref[32:32 + rows, :], ext_ref[0:rows, :])

    k = lax.broadcasted_iota(jnp.int32, (rows, lanes), 1)
    y = (k >> 4) & 15
    eyp = _expand(hyp_ref[...], "y_hi", lanes)
    eym = _expand(hym_ref[...], "y_lo", lanes)
    yp1 = jnp.where(y == 15, pltpu.roll(eyp, 16, 1), pltpu.roll(cur, lanes - 16, 1))
    yp2 = jnp.where(y >= 14, eyp, pltpu.roll(cur, lanes - 32, 1))
    ym1 = jnp.where(y == 0, pltpu.roll(eym, lanes - 16, 1), pltpu.roll(cur, 16, 1))
    ym2 = jnp.where(y <= 1, eym, pltpu.roll(cur, 32, 1))
    dy = _deriv(yp1, ym1, yp2, ym2)

    drift = fx_ref[...] * dx
    a_ref[...] = drift + fy_ref[...] * dy
    q_ref[...] = rate_ref[...] * cur


def _full(shape):
    zeros = (0,) * len(shape)
    return pl.BlockSpec(shape, lambda *_: zeros)


def _send_shape(lanes, peers, both):
    return jax.ShapeDtypeStruct((peers * both, lanes), BF16)


def _send(pick, rnd, peers, both):
    shape = _send_shape(rnd.shape[1], peers, both)
    return pl.pallas_call(_send_kernel, out_shape=shape)(pick, rnd)


def _halos(cur):
    halo = jax.ShapeDtypeStruct((cur.shape[0], 128), F32)
    return pl.pallas_call(_halo_kernel, out_shape=[halo] * 4)(cur)


def _finish(last, pick, sel, inc, cur, a, q, fz, hzp, hzm, tiles, peers, both):
    rows, lanes = cur.shape
    tile_count = tiles.shape[0]
    shapes = [jax.ShapeDtypeStruct((rows, lanes), F32)]
    if not last:
        shapes.append(_send_shape(lanes, peers, both))
    small = (pick, sel, inc, cur, a, q, fz, hzp, hzm)
    outs = pl.pallas_call(
        functools.partial(_finish_kernel, last),
        out_shape=shapes,
        grid=(tile_count,),
        in_specs=[_full(x.shape) for x in small]
        + [pl.BlockSpec((1,) + tiles.shape[1:], lambda t: (t, 0, 0))],
        out_specs=[_full(x.shape) for x in shapes],
        scratch_shapes=[
            pltpu.VMEM((tile_count * rows, lanes), BF16),
            pltpu.VMEM((rows, lanes), F32),
            pltpu.VMEM((rows, lanes), F32),
        ],
        compiler_params=pltpu.CompilerParams(dimension_semantics=("arbitrary",)),
    )(*small, tiles)
    return outs[0], outs[1:]


def _drift(cur, xlo, xhi, hyp, hym, fx, fy, rate):
    rows, lanes = cur.shape
    plane = jax.ShapeDtypeStruct((rows, lanes), F32)
    return pl.pallas_call(
        _drift_kernel,
        out_shape=[plane, plane],
        scratch_shapes=[pltpu.VMEM((rows + 32, lanes), F32)],
    )(cur, xlo, xhi, hyp, hym, fx, fy, rate)


def _ring(axis):
    size = lax.axis_size(axis)
    up = [(i, (i + 1) % size) for i in range(size)]
    down = [(j, i) for i, j in up]
    return up, down


def per_device(populations, force, rate, tiles, send_planes, recv_target, recv_tile, recv_count):
    width_x, drive_count, band_count, width_y, width_z = populations.shape
    rows = width_x * drive_count
    lanes = band_count * width_y * width_z
    peer_count = lax.axis_size("kz")
    slot_cap = send_planes.shape[-1]
    tile_count = tiles.shape[0]
    plane_list = send_planes.reshape(peer_count * slot_cap)
    slot_count = recv_count.reshape(peer_count)
    target_ids = recv_target.reshape(peer_count, slot_cap)
    tile_ids = recv_tile.reshape(peer_count, slot_cap)
    usable = lax.broadcasted_iota(jnp.int32, (peer_count, slot_cap), 1) < slot_count[:, None]
    tile_match = (
        tile_ids[None, None] == jnp.arange(tile_count, dtype=jnp.int32)[:, None, None, None]
    )
    plane_match = (
        target_ids[None, None] == jnp.arange(width_x, dtype=jnp.int32)[None, :, None, None]
    )
    selector = (tile_match & plane_match & usable[None, None]).astype(BF16)
    flat_tile = jnp.repeat(tile_ids.reshape(-1), drive_count)
    flat_target = jnp.repeat(target_ids.reshape(-1), drive_count)
    flat_usable = jnp.repeat(usable.reshape(-1), drive_count)
    big_rows = tile_count * width_x * drive_count
    big_cols = peer_count * slot_cap * drive_count
    r = lax.broadcasted_iota(jnp.int32, (big_rows, big_cols), 0)
    col = lax.broadcasted_iota(jnp.int32, (big_rows, big_cols), 1)
    hit = (r // (width_x * drive_count)) == flat_tile[None, :]
    hit = hit & (((r // drive_count) % width_x) == flat_target[None, :])
    hit = hit & flat_usable[None, :] & ((r % drive_count) == (col % drive_count))
    sel_big = hit.astype(BF16)
    both = slot_cap * drive_count
    flat_plane = jnp.repeat(plane_list, drive_count)
    pr = lax.broadcasted_iota(jnp.int32, (peer_count * both, rows), 0)
    pc = lax.broadcasted_iota(jnp.int32, (peer_count * both, rows), 1)
    pick = ((flat_plane[:, None] == pc // drive_count) & (pr % drive_count == pc % drive_count)).astype(BF16)

    def spread(a):
        a = a.reshape(width_x, 1, lanes)
        return jnp.broadcast_to(a, (width_x, drive_count, lanes)).reshape(rows, lanes)

    fx = spread(force[:, 0])
    fy = spread(force[:, 1])
    fz = spread(force[:, 2])
    rate_wide = spread(rate)

    up_x, down_x = _ring("kx")
    up_y, down_y = _ring("ky")
    up_z, down_z = _ring("kz")

    snd = _send(pick, populations.astype(BF16).reshape(rows, lanes), peer_count, both)
    _, later = lax.optimization_barrier((snd, populations))
    cur = later.reshape(rows, lanes)
    for iteration in range(ITERS):
        last = iteration + 1 == ITERS
        zlo, zhi, ylo, yhi = _halos(cur)
        xlo = lax.ppermute(cur[rows - 16:], "kx", up_x)
        xhi = lax.ppermute(cur[:16], "kx", down_x)
        hym = lax.ppermute(yhi, "ky", up_y)
        hyp = lax.ppermute(ylo, "ky", down_y)
        hzm = lax.ppermute(zhi, "kz", up_z)
        hzp = lax.ppermute(zlo, "kz", down_z)
        outgoing = snd.reshape(peer_count, both, lanes)
        incoming = lax.all_to_all(outgoing, "kz", split_axis=0, concat_axis=0, tiled=True)
        a, q = _drift(cur, xlo, xhi, hyp, hym, fx, fy, rate_wide)
        inc = incoming.reshape(peer_count * both, lanes)
        cur, rest = _finish(
            last, pick, sel_big, inc, cur, a, q, fz, hzp, hzm, tiles, peer_count, both
        )
        if not last:
            (snd,) = rest
    return cur.reshape(width_x, drive_count, band_count, width_y, width_z)


def solution(mesh):
    placed = (
        P("kx", None, None, "ky", "kz"),
        P("kx", None, None, "ky", "kz"),
        P("kx", None, "ky", "kz"),
        P(),
        P("kx", "ky", "kz", None, None),
        P("kx", "ky", "kz", None, None),
        P("kx", "ky", "kz", None, None),
        P("kx", "ky", "kz", None),
    )
    return jax.shard_map(
        per_device,
        mesh=mesh,
        in_specs=placed,
        out_specs=P("kx", None, None, "ky", "kz"),
        check_vma=False,
    )
```

```python
import functools

import jax
import jax.numpy as jnp
from jax import lax
from jax.experimental import pallas as pl
from jax.experimental.pallas import tpu as pltpu
from jax.sharding import PartitionSpec as P

ITERS = 2
F32 = jnp.float32
BF16 = jnp.bfloat16


def _split3(h):
    hi = h.astype(BF16)
    rest = h - hi.astype(F32)
    mid = rest.astype(BF16)
    lo = (rest - mid.astype(F32)).astype(BF16)
    return hi, mid, lo


def _exact_dot(h, m):
    hi, mid, lo = _split3(h)
    out = jnp.dot(hi, m, preferred_element_type=F32)
    out = out + jnp.dot(mid, m, preferred_element_type=F32)
    return out + jnp.dot(lo, m, preferred_element_type=F32)


def _select(kind, shape, k_axis):
    k = lax.broadcasted_iota(jnp.int32, shape, k_axis)
    c = lax.broadcasted_iota(jnp.int32, shape, 1 - k_axis)
    z = k & 15
    y = (k >> 4) & 15
    g = k >> 4
    b = k >> 8
    if kind == "z_lo":
        hit = (z < 2) & (c == g * 2 + z)
    elif kind == "z_hi":
        hit = (z >= 14) & (c == g * 2 + z - 14)
    elif kind == "y_lo":
        hit = (y < 2) & (c == b * 32 + y * 16 + z)
    else:
        hit = (y >= 14) & (c == b * 32 + (y - 14) * 16 + z)
    return jnp.where(hit, 1.0, 0.0).astype(BF16)


def _compress(cur, kind):
    lanes = cur.shape[1]
    return _exact_dot(cur, _select(kind, (lanes, 128), 0))


def _expand(h, kind, lanes):
    return _exact_dot(h, _select(kind, (128, lanes), 1))


def _emit_halos(cur, zlo_ref, zhi_ref, ylo_ref, yhi_ref):
    zlo_ref[...] = _compress(cur, "z_lo")
    zhi_ref[...] = _compress(cur, "z_hi")
    ylo_ref[...] = _compress(cur, "y_lo")
    yhi_ref[...] = _compress(cur, "y_hi")


def _emit_send(pick_ref, cur, snd_ref):
    snd_ref[...] = jnp.dot(
        pick_ref[...], cur.astype(BF16), preferred_element_type=F32
    ).astype(BF16)


def _prep_kernel(pick_ref, cur_ref, snd_ref, zlo_ref, zhi_ref, ylo_ref, yhi_ref):
    cur = cur_ref[...]
    _emit_send(pick_ref, cur, snd_ref)
    _emit_halos(cur, zlo_ref, zhi_ref, ylo_ref, yhi_ref)


def _halo_kernel(cur_ref, zlo_ref, zhi_ref, ylo_ref, yhi_ref):
    _emit_halos(cur_ref[...], zlo_ref, zhi_ref, ylo_ref, yhi_ref)


def _finish_kernel(last, pick_ref, sel_ref, inc_ref, cur_ref, a_ref, q_ref, fz_ref,
                   hzp_ref, hzm_ref, w_ref, *refs):
    if last:
        out_ref, g_scr, acc_scr, p_scr = refs
    else:
        out_ref, snd_ref, g_scr, acc_scr, p_scr = refs
    t = pl.program_id(0)
    h = pl.program_id(1)
    rows, _ = cur_ref.shape
    width = w_ref.shape[1]

    @pl.when((t == 0) & (h == 0))
    def _():
        summed = jnp.dot(sel_ref[...], inc_ref[...], preferred_element_type=F32)
        g_scr[...] = summed.astype(BF16)
        acc_scr[...] = jnp.zeros_like(acc_scr)
        cur = cur_ref[...]
        dz = _deriv_z(cur, hzp_ref[...], hzm_ref[...])
        drift = a_ref[...] + fz_ref[...] * dz
        p_scr[...] = cur - drift

    grouped = g_scr[pl.ds(pl.multiple_of(t * rows, rows), rows), :]
    cols = pl.ds(pl.multiple_of(h * width, width), width)
    acc_scr[:, cols] += lax.dot_general(
        grouped, w_ref[0], (((1,), (1,)), ((), ())), preferred_element_type=F32
    )

    @pl.when((t == pl.num_programs(0) - 1) & (h == pl.num_programs(1) - 1))
    def _():
        cur = (p_scr[...] + acc_scr[...]) - q_ref[...]
        out_ref[...] = cur
        if not last:
            _emit_send(pick_ref, cur, snd_ref)


def _deriv(a1, m1, a2, m2):
    return (8.0 * (a1 - m1) - (a2 - m2)) / 12.0


def _deriv_z(cur, hzp, hzm):
    rows, lanes = cur.shape
    z = lax.broadcasted_iota(jnp.int32, (rows, lanes), 1) & 15
    ezp = _expand(hzp, "z_hi", lanes)
    ezm = _expand(hzm, "z_lo", lanes)
    zp1 = jnp.where(z == 15, pltpu.roll(ezp, 1, 1), pltpu.roll(cur, lanes - 1, 1))
    zp2 = jnp.where(z >= 14, ezp, pltpu.roll(cur, lanes - 2, 1))
    zm1 = jnp.where(z == 0, pltpu.roll(ezm, lanes - 1, 1), pltpu.roll(cur, 1, 1))
    zm2 = jnp.where(z <= 1, ezm, pltpu.roll(cur, 2, 1))
    return _deriv(zp1, zm1, zp2, zm2)


def _drift_kernel(cur_ref, xlo_ref, xhi_ref, hyp_ref, hym_ref,
                  fx_ref, fy_ref, rate_ref, a_ref, q_ref, ext_ref):
    rows, lanes = cur_ref.shape
    cur = cur_ref[...]
    ext_ref[0:16, :] = xlo_ref[...]
    ext_ref[16:16 + rows, :] = cur
    ext_ref[16 + rows:32 + rows, :] = xhi_ref[...]
    dx = _deriv(ext_ref[24:24 + rows, :], ext_ref[8:8 + rows, :],
                ext_ref[32:32 + rows, :], ext_ref[0:rows, :])

    k = lax.broadcasted_iota(jnp.int32, (rows, lanes), 1)
    y = (k >> 4) & 15
    eyp = _expand(hyp_ref[...], "y_hi", lanes)
    eym = _expand(hym_ref[...], "y_lo", lanes)
    yp1 = jnp.where(y == 15, pltpu.roll(eyp, 16, 1), pltpu.roll(cur, lanes - 16, 1))
    yp2 = jnp.where(y >= 14, eyp, pltpu.roll(cur, lanes - 32, 1))
    ym1 = jnp.where(y == 0, pltpu.roll(eym, lanes - 16, 1), pltpu.roll(cur, 16, 1))
    ym2 = jnp.where(y <= 1, eym, pltpu.roll(cur, 32, 1))
    dy = _deriv(yp1, ym1, yp2, ym2)

    drift = fx_ref[...] * dx
    a_ref[...] = drift + fy_ref[...] * dy
    q_ref[...] = rate_ref[...] * cur


def _full(shape):
    zeros = (0,) * len(shape)
    return pl.BlockSpec(shape, lambda *_: zeros)


def _send_shape(lanes, peers, both):
    return jax.ShapeDtypeStruct((peers * both, lanes), BF16)


def _prep(pick, cur, peers, both):
    halo = jax.ShapeDtypeStruct((cur.shape[0], 128), F32)
    shapes = [_send_shape(cur.shape[1], peers, both)] + [halo] * 4
    return pl.pallas_call(_prep_kernel, out_shape=shapes)(pick, cur)


def _halos(cur):
    halo = jax.ShapeDtypeStruct((cur.shape[0], 128), F32)
    return pl.pallas_call(_halo_kernel, out_shape=[halo] * 4)(cur)


def _finish(last, pick, sel, inc, cur, a, q, fz, hzp, hzm, tiles, peers, both):
    rows, lanes = cur.shape
    tile_count = tiles.shape[0]
    shapes = [jax.ShapeDtypeStruct((rows, lanes), F32)]
    if not last:
        shapes.append(_send_shape(lanes, peers, both))
    small = (pick, sel, inc, cur, a, q, fz, hzp, hzm)
    halves = 2
    block = (1, tiles.shape[1] // halves, tiles.shape[2])
    outs = pl.pallas_call(
        functools.partial(_finish_kernel, last),
        out_shape=shapes,
        grid=(tile_count, halves),
        in_specs=[_full(x.shape) for x in small]
        + [pl.BlockSpec(block, lambda t, h: (t, h, 0))],
        out_specs=[_full(x.shape) for x in shapes],
        scratch_shapes=[
            pltpu.VMEM((tile_count * rows, lanes), BF16),
            pltpu.VMEM((rows, lanes), F32),
            pltpu.VMEM((rows, lanes), F32),
        ],
        compiler_params=pltpu.CompilerParams(dimension_semantics=("arbitrary", "arbitrary")),
    )(*small, tiles)
    return outs[0], outs[1:]


def _drift(cur, xlo, xhi, hyp, hym, fx, fy, rate):
    rows, lanes = cur.shape
    plane = jax.ShapeDtypeStruct((rows, lanes), F32)
    return pl.pallas_call(
        _drift_kernel,
        out_shape=[plane, plane],
        scratch_shapes=[pltpu.VMEM((rows + 32, lanes), F32)],
    )(cur, xlo, xhi, hyp, hym, fx, fy, rate)


def _ring(axis):
    size = lax.axis_size(axis)
    up = [(i, (i + 1) % size) for i in range(size)]
    down = [(j, i) for i, j in up]
    return up, down


def per_device(populations, force, rate, tiles, send_planes, recv_target, recv_tile, recv_count):
    width_x, drive_count, band_count, width_y, width_z = populations.shape
    rows = width_x * drive_count
    lanes = band_count * width_y * width_z
    peer_count = lax.axis_size("kz")
    slot_cap = send_planes.shape[-1]
    tile_count = tiles.shape[0]
    plane_list = send_planes.reshape(peer_count * slot_cap)
    slot_count = recv_count.reshape(peer_count)
    target_ids = recv_target.reshape(peer_count, slot_cap)
    tile_ids = recv_tile.reshape(peer_count, slot_cap)
    usable = lax.broadcasted_iota(jnp.int32, (peer_count, slot_cap), 1) < slot_count[:, None]
    tile_match = (
        tile_ids[None, None] == jnp.arange(tile_count, dtype=jnp.int32)[:, None, None, None]
    )
    plane_match = (
        target_ids[None, None] == jnp.arange(width_x, dtype=jnp.int32)[None, :, None, None]
    )
    selector = (tile_match & plane_match & usable[None, None]).astype(BF16)
    flat_tile = jnp.repeat(tile_ids.reshape(-1), drive_count)
    flat_target = jnp.repeat(target_ids.reshape(-1), drive_count)
    flat_usable = jnp.repeat(usable.reshape(-1), drive_count)
    big_rows = tile_count * width_x * drive_count
    big_cols = peer_count * slot_cap * drive_count
    r = lax.broadcasted_iota(jnp.int32, (big_rows, big_cols), 0)
    col = lax.broadcasted_iota(jnp.int32, (big_rows, big_cols), 1)
    hit = (r // (width_x * drive_count)) == flat_tile[None, :]
    hit = hit & (((r // drive_count) % width_x) == flat_target[None, :])
    hit = hit & flat_usable[None, :] & ((r % drive_count) == (col % drive_count))
    sel_big = hit.astype(BF16)
    both = slot_cap * drive_count
    flat_plane = jnp.repeat(plane_list, drive_count)
    pr = lax.broadcasted_iota(jnp.int32, (peer_count * both, rows), 0)
    pc = lax.broadcasted_iota(jnp.int32, (peer_count * both, rows), 1)
    pick = ((flat_plane[:, None] == pc // drive_count) & (pr % drive_count == pc % drive_count)).astype(BF16)

    def spread(a):
        a = a.reshape(width_x, 1, lanes)
        return jnp.broadcast_to(a, (width_x, drive_count, lanes)).reshape(rows, lanes)

    fx = spread(force[:, 0])
    fy = spread(force[:, 1])
    fz = spread(force[:, 2])
    rate_wide = spread(rate)

    up_x, down_x = _ring("kx")
    up_y, down_y = _ring("ky")
    up_z, down_z = _ring("kz")

    cur = populations.reshape(rows, lanes)
    snd, zlo, zhi, ylo, yhi = _prep(pick, cur, peer_count, both)
    for iteration in range(ITERS):
        last = iteration + 1 == ITERS
        if iteration > 0:
            zlo, zhi, ylo, yhi = _halos(cur)
        xlo = lax.ppermute(cur[rows - 16:], "kx", up_x)
        xhi = lax.ppermute(cur[:16], "kx", down_x)
        hym = lax.ppermute(yhi, "ky", up_y)
        hyp = lax.ppermute(ylo, "ky", down_y)
        hzm = lax.ppermute(zhi, "kz", up_z)
        hzp = lax.ppermute(zlo, "kz", down_z)
        outgoing = snd.reshape(peer_count, both, lanes)
        incoming = lax.all_to_all(outgoing, "kz", split_axis=0, concat_axis=0, tiled=True)
        a, q = _drift(cur, xlo, xhi, hyp, hym, fx, fy, rate_wide)
        inc = incoming.reshape(peer_count * both, lanes)
        cur, rest = _finish(
            last, pick, sel_big, inc, cur, a, q, fz, hzp, hzm, tiles, peer_count, both
        )
        if not last:
            (snd,) = rest
    return cur.reshape(width_x, drive_count, band_count, width_y, width_z)


def solution(mesh):
    placed = (
        P("kx", None, None, "ky", "kz"),
        P("kx", None, None, "ky", "kz"),
        P("kx", None, "ky", "kz"),
        P(),
        P("kx", "ky", "kz", None, None),
        P("kx", "ky", "kz", None, None),
        P("kx", "ky", "kz", None, None),
        P("kx", "ky", "kz", None),
    )
    return jax.shard_map(
        per_device,
        mesh=mesh,
        in_specs=placed,
        out_specs=P("kx", None, None, "ky", "kz"),
        check_vma=False,
    )
```

```python
import functools

import jax
import jax.numpy as jnp
from jax import lax
from jax.experimental import pallas as pl
from jax.experimental.pallas import tpu as pltpu
from jax.sharding import PartitionSpec as P

ITERS = 2
F32 = jnp.float32
BF16 = jnp.bfloat16


def _split3(h):
    hi = h.astype(BF16)
    rest = h - hi.astype(F32)
    mid = rest.astype(BF16)
    lo = (rest - mid.astype(F32)).astype(BF16)
    return hi, mid, lo


def _exact_dot(h, m):
    hi, mid, lo = _split3(h)
    out = jnp.dot(hi, m, preferred_element_type=F32)
    out = out + jnp.dot(mid, m, preferred_element_type=F32)
    return out + jnp.dot(lo, m, preferred_element_type=F32)


def _select(kind, shape, k_axis):
    k = lax.broadcasted_iota(jnp.int32, shape, k_axis)
    c = lax.broadcasted_iota(jnp.int32, shape, 1 - k_axis)
    z = k & 15
    y = (k >> 4) & 15
    g = k >> 4
    b = k >> 8
    if kind == "z_lo":
        hit = (z < 2) & (c == g * 2 + z)
    elif kind == "z_hi":
        hit = (z >= 14) & (c == g * 2 + z - 14)
    elif kind == "y_lo":
        hit = (y < 2) & (c == b * 32 + y * 16 + z)
    else:
        hit = (y >= 14) & (c == b * 32 + (y - 14) * 16 + z)
    return jnp.where(hit, 1.0, 0.0).astype(BF16)


def _compress(cur, kind):
    lanes = cur.shape[1]
    return _exact_dot(cur, _select(kind, (lanes, 128), 0))


def _expand(h, kind, lanes):
    return _exact_dot(h, _select(kind, (128, lanes), 1))


def _emit_halos(cur, zlo_ref, zhi_ref, ylo_ref, yhi_ref):
    zlo_ref[...] = _compress(cur, "z_lo")
    zhi_ref[...] = _compress(cur, "z_hi")
    ylo_ref[...] = _compress(cur, "y_lo")
    yhi_ref[...] = _compress(cur, "y_hi")


def _emit_send(pick_ref, cur, snd_ref):
    snd_ref[...] = jnp.dot(
        pick_ref[...], cur.astype(BF16), preferred_element_type=F32
    ).astype(BF16)


def _send_kernel(pick_ref, cur_ref, snd_ref):
    _emit_send(pick_ref, cur_ref[...], snd_ref)


def _halo_kernel(cur_ref, zlo_ref, zhi_ref, ylo_ref, yhi_ref):
    _emit_halos(cur_ref[...], zlo_ref, zhi_ref, ylo_ref, yhi_ref)


def _finish_kernel(last, pick_ref, sel_ref, inc_ref, cur_ref, a_ref, q_ref, fz_ref,
                   hzp_ref, hzm_ref, w_ref, *refs):
    if last:
        out_ref, g_scr, acc_scr, p_scr = refs
    else:
        out_ref, snd_ref, g_scr, acc_scr, p_scr = refs
    t = pl.program_id(0)
    rows, _ = cur_ref.shape

    @pl.when(t == 0)
    def _():
        summed = jnp.dot(sel_ref[...], inc_ref[...], preferred_element_type=F32)
        g_scr[...] = summed.astype(BF16)
        acc_scr[...] = jnp.zeros_like(acc_scr)
        cur = cur_ref[...]
        dz = _deriv_z(cur, hzp_ref[...], hzm_ref[...])
        drift = a_ref[...] + fz_ref[...] * dz
        p_scr[...] = cur - drift

    grouped = g_scr[pl.ds(pl.multiple_of(t * rows, rows), rows), :]
    acc_scr[...] += lax.dot_general(
        grouped, w_ref[0], (((1,), (1,)), ((), ())), preferred_element_type=F32
    )

    @pl.when(t == pl.num_programs(0) - 1)
    def _():
        cur = (p_scr[...] + acc_scr[...]) - q_ref[...]
        out_ref[...] = cur
        if not last:
            _emit_send(pick_ref, cur, snd_ref)


def _deriv(a1, m1, a2, m2):
    return (8.0 * (a1 - m1) - (a2 - m2)) / 12.0


def _deriv_z(cur, hzp, hzm):
    rows, lanes = cur.shape
    z = lax.broadcasted_iota(jnp.int32, (rows, lanes), 1) & 15
    ezp = _expand(hzp, "z_hi", lanes)
    ezm = _expand(hzm, "z_lo", lanes)
    zp1 = jnp.where(z == 15, pltpu.roll(ezp, 1, 1), pltpu.roll(cur, lanes - 1, 1))
    zp2 = jnp.where(z >= 14, ezp, pltpu.roll(cur, lanes - 2, 1))
    zm1 = jnp.where(z == 0, pltpu.roll(ezm, lanes - 1, 1), pltpu.roll(cur, 1, 1))
    zm2 = jnp.where(z <= 1, ezm, pltpu.roll(cur, 2, 1))
    return _deriv(zp1, zm1, zp2, zm2)


def _drift_kernel(cur_ref, xlo_ref, xhi_ref, hyp_ref, hym_ref,
                  fx_ref, fy_ref, rate_ref, a_ref, q_ref, ext_ref):
    rows, lanes = cur_ref.shape
    cur = cur_ref[...]
    ext_ref[0:16, :] = xlo_ref[...]
    ext_ref[16:16 + rows, :] = cur
    ext_ref[16 + rows:32 + rows, :] = xhi_ref[...]
    dx = _deriv(ext_ref[24:24 + rows, :], ext_ref[8:8 + rows, :],
                ext_ref[32:32 + rows, :], ext_ref[0:rows, :])

    k = lax.broadcasted_iota(jnp.int32, (rows, lanes), 1)
    y = (k >> 4) & 15
    eyp = _expand(hyp_ref[...], "y_hi", lanes)
    eym = _expand(hym_ref[...], "y_lo", lanes)
    yp1 = jnp.where(y == 15, pltpu.roll(eyp, 16, 1), pltpu.roll(cur, lanes - 16, 1))
    yp2 = jnp.where(y >= 14, eyp, pltpu.roll(cur, lanes - 32, 1))
    ym1 = jnp.where(y == 0, pltpu.roll(eym, lanes - 16, 1), pltpu.roll(cur, 16, 1))
    ym2 = jnp.where(y <= 1, eym, pltpu.roll(cur, 32, 1))
    dy = _deriv(yp1, ym1, yp2, ym2)

    drift = fx_ref[...] * dx
    a_ref[...] = drift + fy_ref[...] * dy
    q_ref[...] = rate_ref[...] * cur


def _full(shape):
    zeros = (0,) * len(shape)
    return pl.BlockSpec(shape, lambda *_: zeros)


def _send_shape(lanes, peers, both):
    return jax.ShapeDtypeStruct((peers * both, lanes), BF16)


def _send(pick, cur, peers, both):
    shape = _send_shape(cur.shape[1], peers, both)
    return pl.pallas_call(_send_kernel, out_shape=shape)(pick, cur)


def _halos(cur):
    halo = jax.ShapeDtypeStruct((cur.shape[0], 128), F32)
    return pl.pallas_call(_halo_kernel, out_shape=[halo] * 4)(cur)


def _finish(last, pick, sel, inc, cur, a, q, fz, hzp, hzm, tiles, peers, both):
    rows, lanes = cur.shape
    tile_count = tiles.shape[0]
    shapes = [jax.ShapeDtypeStruct((rows, lanes), F32)]
    if not last:
        shapes.append(_send_shape(lanes, peers, both))
    small = (pick, sel, inc, cur, a, q, fz, hzp, hzm)
    outs = pl.pallas_call(
        functools.partial(_finish_kernel, last),
        out_shape=shapes,
        grid=(tile_count,),
        in_specs=[_full(x.shape) for x in small]
        + [pl.BlockSpec((1,) + tiles.shape[1:], lambda t: (t, 0, 0))],
        out_specs=[_full(x.shape) for x in shapes],
        scratch_shapes=[
            pltpu.VMEM((tile_count * rows, lanes), BF16),
            pltpu.VMEM((rows, lanes), F32),
            pltpu.VMEM((rows, lanes), F32),
        ],
        compiler_params=pltpu.CompilerParams(dimension_semantics=("arbitrary",)),
    )(*small, tiles)
    return outs[0], outs[1:]


def _drift(cur, xlo, xhi, hyp, hym, fx, fy, rate):
    rows, lanes = cur.shape
    plane = jax.ShapeDtypeStruct((rows, lanes), F32)
    return pl.pallas_call(
        _drift_kernel,
        out_shape=[plane, plane],
        scratch_shapes=[pltpu.VMEM((rows + 32, lanes), F32)],
    )(cur, xlo, xhi, hyp, hym, fx, fy, rate)


def _ring(axis):
    size = lax.axis_size(axis)
    up = [(i, (i + 1) % size) for i in range(size)]
    down = [(j, i) for i, j in up]
    return up, down


def per_device(populations, force, rate, tiles, send_planes, recv_target, recv_tile, recv_count):
    width_x, drive_count, band_count, width_y, width_z = populations.shape
    rows = width_x * drive_count
    lanes = band_count * width_y * width_z
    peer_count = lax.axis_size("kz")
    slot_cap = send_planes.shape[-1]
    tile_count = tiles.shape[0]
    plane_list = send_planes.reshape(peer_count * slot_cap)
    slot_count = recv_count.reshape(peer_count)
    target_ids = recv_target.reshape(peer_count, slot_cap)
    tile_ids = recv_tile.reshape(peer_count, slot_cap)
    usable = lax.broadcasted_iota(jnp.int32, (peer_count, slot_cap), 1) < slot_count[:, None]
    tile_match = (
        tile_ids[None, None] == jnp.arange(tile_count, dtype=jnp.int32)[:, None, None, None]
    )
    plane_match = (
        target_ids[None, None] == jnp.arange(width_x, dtype=jnp.int32)[None, :, None, None]
    )
    selector = (tile_match & plane_match & usable[None, None]).astype(BF16)
    flat_tile = jnp.repeat(tile_ids.reshape(-1), drive_count)
    flat_target = jnp.repeat(target_ids.reshape(-1), drive_count)
    flat_usable = jnp.repeat(usable.reshape(-1), drive_count)
    big_rows = tile_count * width_x * drive_count
    big_cols = peer_count * slot_cap * drive_count
    r = lax.broadcasted_iota(jnp.int32, (big_rows, big_cols), 0)
    col = lax.broadcasted_iota(jnp.int32, (big_rows, big_cols), 1)
    hit = (r // (width_x * drive_count)) == flat_tile[None, :]
    hit = hit & (((r // drive_count) % width_x) == flat_target[None, :])
    hit = hit & flat_usable[None, :] & ((r % drive_count) == (col % drive_count))
    sel_big = hit.astype(BF16)
    both = slot_cap * drive_count
    flat_plane = jnp.repeat(plane_list, drive_count)
    pr = lax.broadcasted_iota(jnp.int32, (peer_count * both, rows), 0)
    pc = lax.broadcasted_iota(jnp.int32, (peer_count * both, rows), 1)
    pick = ((flat_plane[:, None] == pc // drive_count) & (pr % drive_count == pc % drive_count)).astype(BF16)

    def spread(a):
        a = a.reshape(width_x, 1, lanes)
        return jnp.broadcast_to(a, (width_x, drive_count, lanes)).reshape(rows, lanes)

    fx = spread(force[:, 0])
    fy = spread(force[:, 1])
    fz = spread(force[:, 2])
    rate_wide = spread(rate)

    up_x, down_x = _ring("kx")
    up_y, down_y = _ring("ky")
    up_z, down_z = _ring("kz")

    cur = populations.reshape(rows, lanes)
    snd = _send(pick, cur, peer_count, both)
    _, cur_late = lax.optimization_barrier((snd, cur))
    for iteration in range(ITERS):
        last = iteration + 1 == ITERS
        zlo, zhi, ylo, yhi = _halos(cur_late if iteration == 0 else cur)
        xlo = lax.ppermute(cur[rows - 16:], "kx", up_x)
        xhi = lax.ppermute(cur[:16], "kx", down_x)
        hym = lax.ppermute(yhi, "ky", up_y)
        hyp = lax.ppermute(ylo, "ky", down_y)
        hzm = lax.ppermute(zhi, "kz", up_z)
        hzp = lax.ppermute(zlo, "kz", down_z)
        outgoing = snd.reshape(peer_count, both, lanes)
        incoming = lax.all_to_all(outgoing, "kz", split_axis=0, concat_axis=0, tiled=True)
        a, q = _drift(cur, xlo, xhi, hyp, hym, fx, fy, rate_wide)
        inc = incoming.reshape(peer_count * both, lanes)
        cur, rest = _finish(
            last, pick, sel_big, inc, cur, a, q, fz, hzp, hzm, tiles, peer_count, both
        )
        if not last:
            (snd,) = rest
    return cur.reshape(width_x, drive_count, band_count, width_y, width_z)


def solution(mesh):
    placed = (
        P("kx", None, None, "ky", "kz"),
        P("kx", None, None, "ky", "kz"),
        P("kx", None, "ky", "kz"),
        P(),
        P("kx", "ky", "kz", None, None),
        P("kx", "ky", "kz", None, None),
        P("kx", "ky", "kz", None, None),
        P("kx", "ky", "kz", None),
    )
    return jax.shard_map(
        per_device,
        mesh=mesh,
        in_specs=placed,
        out_specs=P("kx", None, None, "ky", "kz"),
        check_vma=False,
    )
```

```python
import functools

import jax
import jax.numpy as jnp
from jax import lax
from jax.experimental import pallas as pl
from jax.experimental.pallas import tpu as pltpu
from jax.sharding import PartitionSpec as P

ITERS = 2
F32 = jnp.float32
BF16 = jnp.bfloat16


def _split3(h):
    hi = h.astype(BF16)
    rest = h - hi.astype(F32)
    mid = rest.astype(BF16)
    lo = (rest - mid.astype(F32)).astype(BF16)
    return hi, mid, lo


def _exact_dot(h, m):
    hi, mid, lo = _split3(h)
    out = jnp.dot(hi, m, preferred_element_type=F32)
    out = out + jnp.dot(mid, m, preferred_element_type=F32)
    return out + jnp.dot(lo, m, preferred_element_type=F32)


def _select(kind, shape, k_axis):
    k = lax.broadcasted_iota(jnp.int32, shape, k_axis)
    c = lax.broadcasted_iota(jnp.int32, shape, 1 - k_axis)
    z = k & 15
    y = (k >> 4) & 15
    g = k >> 4
    b = k >> 8
    if kind == "z_lo":
        hit = (z < 2) & (c == g * 2 + z)
    elif kind == "z_hi":
        hit = (z >= 14) & (c == g * 2 + z - 14)
    elif kind == "y_lo":
        hit = (y < 2) & (c == b * 32 + y * 16 + z)
    else:
        hit = (y >= 14) & (c == b * 32 + (y - 14) * 16 + z)
    return jnp.where(hit, 1.0, 0.0).astype(BF16)


def _compress(cur, kind):
    lanes = cur.shape[1]
    return _exact_dot(cur, _select(kind, (lanes, 128), 0))


def _expand(h, kind, lanes):
    return _exact_dot(h, _select(kind, (128, lanes), 1))


def _emit_halos(cur, zlo_ref, zhi_ref, ylo_ref, yhi_ref):
    zlo_ref[...] = _compress(cur, "z_lo")
    zhi_ref[...] = _compress(cur, "z_hi")
    ylo_ref[...] = _compress(cur, "y_lo")
    yhi_ref[...] = _compress(cur, "y_hi")


def _emit_send(pick_ref, cur, snd_ref):
    rows = cur.shape[0]
    shape = (pick_ref.shape[0], rows)
    pr = lax.broadcasted_iota(jnp.int32, shape, 0)
    pc = lax.broadcasted_iota(jnp.int32, shape, 1)
    hit = (pick_ref[...] == (pc >> 3)) & ((pr & 7) == (pc & 7))
    pick = jnp.where(hit, 1.0, 0.0).astype(BF16)
    snd_ref[...] = jnp.dot(pick, cur.astype(BF16), preferred_element_type=F32).astype(BF16)


def _send_kernel(pick_ref, cur_ref, snd_ref):
    _emit_send(pick_ref, cur_ref[...], snd_ref)


def _halo_kernel(cur_ref, zlo_ref, zhi_ref, ylo_ref, yhi_ref):
    _emit_halos(cur_ref[...], zlo_ref, zhi_ref, ylo_ref, yhi_ref)


def _finish_kernel(last, pick_ref, sel_ref, inc_ref, cur_ref, a_ref, q_ref, fz_ref,
                   hzp_ref, hzm_ref, w_ref, *refs):
    if last:
        out_ref, g_scr, acc_scr, p_scr = refs
    else:
        out_ref, snd_ref, g_scr, acc_scr, p_scr = refs
    t = pl.program_id(0)
    rows, _ = cur_ref.shape

    @pl.when(t == 0)
    def _():
        summed = jnp.dot(sel_ref[...], inc_ref[...], preferred_element_type=F32)
        g_scr[...] = summed.astype(BF16)
        acc_scr[...] = jnp.zeros_like(acc_scr)
        cur = cur_ref[...]
        dz = _deriv_z(cur, hzp_ref[...], hzm_ref[...])
        drift = a_ref[...] + fz_ref[...] * dz
        p_scr[...] = cur - drift

    grouped = g_scr[pl.ds(pl.multiple_of(t * rows, rows), rows), :]
    acc_scr[...] += lax.dot_general(
        grouped, w_ref[0], (((1,), (1,)), ((), ())), preferred_element_type=F32
    )

    @pl.when(t == pl.num_programs(0) - 1)
    def _():
        cur = (p_scr[...] + acc_scr[...]) - q_ref[...]
        out_ref[...] = cur
        if not last:
            _emit_send(pick_ref, cur, snd_ref)


def _deriv(a1, m1, a2, m2):
    return (8.0 * (a1 - m1) - (a2 - m2)) / 12.0


def _deriv_z(cur, hzp, hzm):
    rows, lanes = cur.shape
    z = lax.broadcasted_iota(jnp.int32, (rows, lanes), 1) & 15
    ezp = _expand(hzp, "z_hi", lanes)
    ezm = _expand(hzm, "z_lo", lanes)
    zp1 = jnp.where(z == 15, pltpu.roll(ezp, 1, 1), pltpu.roll(cur, lanes - 1, 1))
    zp2 = jnp.where(z >= 14, ezp, pltpu.roll(cur, lanes - 2, 1))
    zm1 = jnp.where(z == 0, pltpu.roll(ezm, lanes - 1, 1), pltpu.roll(cur, 1, 1))
    zm2 = jnp.where(z <= 1, ezm, pltpu.roll(cur, 2, 1))
    return _deriv(zp1, zm1, zp2, zm2)


def _drift_kernel(cur_ref, xlo_ref, xhi_ref, hyp_ref, hym_ref,
                  fx_ref, fy_ref, rate_ref, a_ref, q_ref, ext_ref):
    rows, lanes = cur_ref.shape
    cur = cur_ref[...]
    ext_ref[0:16, :] = xlo_ref[...]
    ext_ref[16:16 + rows, :] = cur
    ext_ref[16 + rows:32 + rows, :] = xhi_ref[...]
    dx = _deriv(ext_ref[24:24 + rows, :], ext_ref[8:8 + rows, :],
                ext_ref[32:32 + rows, :], ext_ref[0:rows, :])

    k = lax.broadcasted_iota(jnp.int32, (rows, lanes), 1)
    y = (k >> 4) & 15
    eyp = _expand(hyp_ref[...], "y_hi", lanes)
    eym = _expand(hym_ref[...], "y_lo", lanes)
    yp1 = jnp.where(y == 15, pltpu.roll(eyp, 16, 1), pltpu.roll(cur, lanes - 16, 1))
    yp2 = jnp.where(y >= 14, eyp, pltpu.roll(cur, lanes - 32, 1))
    ym1 = jnp.where(y == 0, pltpu.roll(eym, lanes - 16, 1), pltpu.roll(cur, 16, 1))
    ym2 = jnp.where(y <= 1, eym, pltpu.roll(cur, 32, 1))
    dy = _deriv(yp1, ym1, yp2, ym2)

    drift = fx_ref[...] * dx
    a_ref[...] = drift + fy_ref[...] * dy
    q_ref[...] = rate_ref[...] * cur


def _full(shape):
    zeros = (0,) * len(shape)
    return pl.BlockSpec(shape, lambda *_: zeros)


def _send_shape(lanes, peers, both):
    return jax.ShapeDtypeStruct((peers * both, lanes), BF16)


def _send(pick, cur, peers, both):
    shape = _send_shape(cur.shape[1], peers, both)
    return pl.pallas_call(_send_kernel, out_shape=shape)(pick, cur)


def _halos(cur):
    halo = jax.ShapeDtypeStruct((cur.shape[0], 128), F32)
    return pl.pallas_call(_halo_kernel, out_shape=[halo] * 4)(cur)


def _finish(last, pick, sel, inc, cur, a, q, fz, hzp, hzm, tiles, peers, both):
    rows, lanes = cur.shape
    tile_count = tiles.shape[0]
    shapes = [jax.ShapeDtypeStruct((rows, lanes), F32)]
    if not last:
        shapes.append(_send_shape(lanes, peers, both))
    small = (pick, sel, inc, cur, a, q, fz, hzp, hzm)
    outs = pl.pallas_call(
        functools.partial(_finish_kernel, last),
        out_shape=shapes,
        grid=(tile_count,),
        in_specs=[_full(x.shape) for x in small]
        + [pl.BlockSpec((1,) + tiles.shape[1:], lambda t: (t, 0, 0))],
        out_specs=[_full(x.shape) for x in shapes],
        scratch_shapes=[
            pltpu.VMEM((tile_count * rows, lanes), BF16),
            pltpu.VMEM((rows, lanes), F32),
            pltpu.VMEM((rows, lanes), F32),
        ],
        compiler_params=pltpu.CompilerParams(dimension_semantics=("arbitrary",)),
    )(*small, tiles)
    return outs[0], outs[1:]


def _drift(cur, xlo, xhi, hyp, hym, fx, fy, rate):
    rows, lanes = cur.shape
    plane = jax.ShapeDtypeStruct((rows, lanes), F32)
    return pl.pallas_call(
        _drift_kernel,
        out_shape=[plane, plane],
        scratch_shapes=[pltpu.VMEM((rows + 32, lanes), F32)],
    )(cur, xlo, xhi, hyp, hym, fx, fy, rate)


def _ring(axis):
    size = lax.axis_size(axis)
    up = [(i, (i + 1) % size) for i in range(size)]
    down = [(j, i) for i, j in up]
    return up, down


def per_device(populations, force, rate, tiles, send_planes, recv_target, recv_tile, recv_count):
    width_x, drive_count, band_count, width_y, width_z = populations.shape
    rows = width_x * drive_count
    lanes = band_count * width_y * width_z
    peer_count = lax.axis_size("kz")
    slot_cap = send_planes.shape[-1]
    tile_count = tiles.shape[0]
    plane_list = send_planes.reshape(peer_count * slot_cap)
    slot_count = recv_count.reshape(peer_count)
    target_ids = recv_target.reshape(peer_count, slot_cap)
    tile_ids = recv_tile.reshape(peer_count, slot_cap)
    usable = lax.broadcasted_iota(jnp.int32, (peer_count, slot_cap), 1) < slot_count[:, None]
    tile_match = (
        tile_ids[None, None] == jnp.arange(tile_count, dtype=jnp.int32)[:, None, None, None]
    )
    plane_match = (
        target_ids[None, None] == jnp.arange(width_x, dtype=jnp.int32)[None, :, None, None]
    )
    selector = (tile_match & plane_match & usable[None, None]).astype(BF16)
    flat_tile = jnp.repeat(tile_ids.reshape(-1), drive_count)
    flat_target = jnp.repeat(target_ids.reshape(-1), drive_count)
    flat_usable = jnp.repeat(usable.reshape(-1), drive_count)
    big_rows = tile_count * width_x * drive_count
    big_cols = peer_count * slot_cap * drive_count
    r = lax.broadcasted_iota(jnp.int32, (big_rows, big_cols), 0)
    col = lax.broadcasted_iota(jnp.int32, (big_rows, big_cols), 1)
    hit = (r // (width_x * drive_count)) == flat_tile[None, :]
    hit = hit & (((r // drive_count) % width_x) == flat_target[None, :])
    hit = hit & flat_usable[None, :] & ((r % drive_count) == (col % drive_count))
    sel_big = hit.astype(BF16)
    both = slot_cap * drive_count
    flat_plane = jnp.repeat(plane_list, drive_count)
    pick = flat_plane.reshape(peer_count * both, 1)

    def spread(a):
        a = a.reshape(width_x, 1, lanes)
        return jnp.broadcast_to(a, (width_x, drive_count, lanes)).reshape(rows, lanes)

    fx = spread(force[:, 0])
    fy = spread(force[:, 1])
    fz = spread(force[:, 2])
    rate_wide = spread(rate)

    up_x, down_x = _ring("kx")
    up_y, down_y = _ring("ky")
    up_z, down_z = _ring("kz")

    cur = populations.reshape(rows, lanes)
    snd = _send(pick, cur, peer_count, both)
    _, cur_late = lax.optimization_barrier((snd, cur))
    for iteration in range(ITERS):
        last = iteration + 1 == ITERS
        zlo, zhi, ylo, yhi = _halos(cur_late if iteration == 0 else cur)
        xlo = lax.ppermute(cur[rows - 16:], "kx", up_x)
        xhi = lax.ppermute(cur[:16], "kx", down_x)
        hym = lax.ppermute(yhi, "ky", up_y)
        hyp = lax.ppermute(ylo, "ky", down_y)
        hzm = lax.ppermute(zhi, "kz", up_z)
        hzp = lax.ppermute(zlo, "kz", down_z)
        outgoing = snd.reshape(peer_count, both, lanes)
        incoming = lax.all_to_all(outgoing, "kz", split_axis=0, concat_axis=0, tiled=True)
        a, q = _drift(cur, xlo, xhi, hyp, hym, fx, fy, rate_wide)
        inc = incoming.reshape(peer_count * both, lanes)
        cur, rest = _finish(
            last, pick, sel_big, inc, cur, a, q, fz, hzp, hzm, tiles, peer_count, both
        )
        if not last:
            (snd,) = rest
    return cur.reshape(width_x, drive_count, band_count, width_y, width_z)


def solution(mesh):
    placed = (
        P("kx", None, None, "ky", "kz"),
        P("kx", None, None, "ky", "kz"),
        P("kx", None, "ky", "kz"),
        P(),
        P("kx", "ky", "kz", None, None),
        P("kx", "ky", "kz", None, None),
        P("kx", "ky", "kz", None, None),
        P("kx", "ky", "kz", None),
    )
    return jax.shard_map(
        per_device,
        mesh=mesh,
        in_specs=placed,
        out_specs=P("kx", None, None, "ky", "kz"),
        check_vma=False,
    )
```
